512 devices in a mesh: req: 64 (over x, z, core), tp: 8 (over y).
Axes of the slice: x: 4, y: 8, z: 8, core: 2. Of those that a mesh axis runs over, the one named last changes fastest.
Arguments:
- queries: bfloat16 [1280, 2048], P('req', 'tp')
- new_keys: bfloat16 [1280, 2048], P('req', 'tp'), may hold values from -6 to 6
- new_values: bfloat16 [1280, 2048], P('req', 'tp'), may hold values from -6 to 6
- cache_keys: bfloat16 [256, 384, 2048], P('req', None, 'tp'), may hold values from -6 to 6
- cache_values: bfloat16 [256, 384, 2048], P('req', None, 'tp'), may hold values from -6 to 6
- cache_lengths: int32 [256], P('req'), may hold values from 1 to 384, as said below
- hidden_in: bfloat16 [1280, 2048], P('req'), may hold values from -6 to 6
- out_weight: bfloat16 [2048, 2048], P('tp'), may hold values from -0.125 to 0.125
- norm_gain: float32 [2048], replicated, may hold values from 0.25 to 1.75
- routes: int32 [1280, 6], P('req'), may hold values from 0 to 63, all different within a row; in each aligned block of 20 rows (0 to 19, 20 to 39, ...) at most 3 rows name the same one
- route_gates: float32 [1280, 6], P('req'), may hold values from 0.05 to 0.5
- gate_weight: bfloat16 [64, 2048, 1408], P('req', None, 'tp'), may hold values from -0.125 to 0.125
- up_weight: bfloat16 [64, 2048, 1408], P('req', None, 'tp'), may hold values from -0.125 to 0.125
- down_weight: bfloat16 [64, 1408, 2048], P('req', 'tp'), may hold values from -0.15625 to 0.15625
Outputs:
- hidden_out: bfloat16 [1280, 2048], P('req', 'tp')
The draws below stay inside these ranges and needn't reach their ends.
Inputs may be any that keep to these rules, and one draw needn't show every extreme that they name: `cache_lengths`: at least one request has all 384 slots live. `routes`: each token names 6 different experts; within each aligned block of 20 tokens (the tokens of one index of req) no expert is named more than 3 times.
All inputs are finite; a program needn't handle non-finite values.
Results may differ from the reference program's by a relative error of at most 0.008.
Values may be sent and summed in bfloat16 or wider, within the bound.
No kernel may reach another device: no remote copies, remote signals or barrier semaphores. Data moves between devices by JAX's collectives and lax.ppermute only.
A program may use at most 64 MiB of HBM per device.

```python
import math
import jax
import jax.numpy as jnp
import numpy as np
from jax import lax

D = 2048
HEADS = 16
HD = 128
EFF = 1408
EXPERTS = 64
TOPK = 6
POS = 5
CACHE = 384
REQUESTS = 256
TOK_DEV = 20
TOKENS = 1280
CAP = 3


def draw_cache_lengths(key, part):
    draw_key = jax.random.fold_in(key, 11)
    place_key = jax.random.fold_in(key, 12)
    lengths = jax.random.randint(draw_key, (REQUESTS,), 1, CACHE + 1)
    where_full = jax.random.randint(place_key, (), 0, REQUESTS)
    return lengths.at[where_full].set(CACHE).astype(jnp.int32)


def draw_queries(key, part):
    values = jax.random.normal(jax.random.fold_in(key, 21), (TOKENS, HEADS * HD), jnp.float32)
    return values.astype(jnp.bfloat16)


def shard_levels(rng, shape, cuts, low, high):
    level, own = 1.0, jax.random.fold_in(rng, 6)
    for axis_at, parts in cuts:
        draws = jnp.exp(jax.random.uniform(jax.random.fold_in(own, axis_at), (parts,), jnp.float32, low / len(cuts), high / len(cuts)))
        level = level * jnp.repeat(draws, shape[axis_at] // parts).reshape([-1 if axis == axis_at else 1 for axis in range(len(shape))])
    return level


def shared_out(own_key, own, number, rows, amount, top, most, skew):
    sequence = jax.random.permutation(own_key, amount)
    crowded, common = portions_of(amount, rows * top, most, skew, True), portions_of(amount, rows * top, most, skew, False)
    places = jnp.arange(amount)

    def named(sizes, turn):
        used = int((sizes > 0).sum())
        fixed = max(1, used // 4)
        moved = fixed + (places - fixed + turn * (used - fixed)) % max(1, amount - fixed)
        return jnp.zeros((amount,), jnp.int32).at[sequence[jnp.where(places < fixed, places, moved)]].set(jnp.asarray(sizes, jnp.int32))

    sizes = jnp.where(number % 4 == 0, named(crowded, number // 4), named(common, number - number // 4 - 1))
    mixed = jax.random.permutation(jax.random.fold_in(own, 3), amount)
    source_of, sink = mixed[0:amount // 2 * 2:2], mixed[1:amount // 2 * 2:2]
    slack = jnp.minimum(sizes[source_of] - 1, most - sizes[sink]) // 2
    slack = jnp.where((source_of == sequence[0]) | (sink == sequence[0]) | (sizes[sink] == 0), 0, jnp.maximum(slack, 0))
    moved = jax.random.randint(jax.random.fold_in(own, 4), (amount // 2,), 0, 1 << 20) % (slack + 1)
    sizes = sizes.at[source_of].add(-moved).at[sink].add(moved)
    labels = jnp.searchsorted(jnp.cumsum(sizes), jnp.arange(rows * top), side="right").astype(jnp.int32)
    table = labels.reshape(top, rows).T
    table = table[jax.random.permutation(jax.random.fold_in(own, 1), rows)]
    turn = jax.random.randint(jax.random.fold_in(own, 2), (rows, 1), 0, top)
    return jnp.take_along_axis(table, (jnp.arange(top)[None, :] + turn) % top, axis=1)


def portions_of(number_of, total, bound, slope, full):
    weights = [(1 << 20) // math.isqrt(standing ** slope) + 1 for standing in range(1, number_of + 1)]
    largest = bound if full else min(bound, max(-(-total // number_of), total * weights[0] // sum(weights)))
    least = 1 if total - largest >= number_of - 1 else 0
    counts, rest = [largest] + [least] * (number_of - 1), total - largest - least * (number_of - 1)
    while rest > 0:
        candidates = [i for i in range(1, number_of) if counts[i] < largest] or [i for i in range(1, number_of) if counts[i] < bound]
        whole, budget = sum([weights[i] for i in candidates]), rest
        for i in candidates:
            addition = min(bound - counts[i], max(1, budget * weights[i] // whole), rest)
            counts[i] = counts[i] + addition
            rest = rest - addition
    return np.array(counts)


def gaussian(rng, shape, width, bound, shards=(), kind=jnp.bfloat16):
    level = shard_levels(rng, shape, shards, -0.22, 0.18) if shards else 1.0
    array = jax.random.normal(rng, shape, jnp.float32) * width * level
    return jnp.minimum(jnp.maximum(array, -bound), bound).astype(kind)


def setup_inputs(seed: int = 0) -> dict:
    key_of = jax.random.split(jax.random.key(seed), 15)
    queries = draw_queries(jax.random.fold_in(key_of[14], 71), 0)
    new_keys = gaussian(key_of[1], (TOKENS, HEADS * HD), 1.0, 6.0, ((0, 64), (1, 8)))
    new_values = gaussian(key_of[2], (TOKENS, HEADS * HD), 1.0, 6.0, ((0, 64), (1, 8)))
    cache_keys = gaussian(key_of[3], (REQUESTS, CACHE, HEADS * HD), 1.0, 6.0, ((0, 64), (2, 8)))
    cache_values = gaussian(key_of[4], (REQUESTS, CACHE, HEADS * HD), 1.0, 6.0, ((0, 64), (2, 8)))
    cache_lengths = draw_cache_lengths(jax.random.fold_in(key_of[14], 71), 0)
    hidden_in = gaussian(key_of[6], (TOKENS, D), 1.0, 6.0, ((0, 64),))
    out_weight = gaussian(key_of[7], (HEADS * HD, D), (HEADS * HD) ** -0.5, 0.125, ((0, 8),))
    norm_gain = jnp.clip(1.0 + 0.15 * jax.random.normal(key_of[8], (D,), jnp.float32), 0.25, 1.75)
    routes_keys = jax.random.split(jax.random.fold_in(key_of[9], 1), TOKENS // TOK_DEV)
    routes_turns = jax.random.permutation(jax.random.fold_in(key_of[9], 3), TOKENS // TOK_DEV)
    routes = jax.vmap(lambda own, number: shared_out(jax.random.fold_in(key_of[9], 2), own, number, TOK_DEV, EXPERTS, TOPK, CAP, 2))(routes_keys, routes_turns).reshape((TOKENS, TOPK))
    route_gates = jnp.clip(0.05 + 0.45 * jax.random.uniform(key_of[10], (TOKENS, TOPK), jnp.float32) ** shard_levels(key_of[10], (TOKENS, TOPK), ((0, 64),), -0.2, 0.2), 0.05, 0.5)
    gate_weight = gaussian(key_of[11], (EXPERTS, D, EFF), D ** -0.5, 0.125, ((0, 64), (2, 8)))
    up_weight = gaussian(key_of[12], (EXPERTS, D, EFF), D ** -0.5, 0.125, ((0, 64), (2, 8)))
    down_weight = gaussian(key_of[13], (EXPERTS, EFF, D), EFF ** -0.5, 0.15625, ((0, 64), (1, 8)))
    return dict(queries=queries, new_keys=new_keys, new_values=new_values, cache_keys=cache_keys, cache_values=cache_values, cache_lengths=cache_lengths, hidden_in=hidden_in, out_weight=out_weight, norm_gain=norm_gain, routes=routes, route_gates=route_gates, gate_weight=gate_weight, up_weight=up_weight, down_weight=down_weight)


def slot_tables(block_routes, block_gates):
    flat_routes = block_routes.reshape(-1)
    expert_ids = jnp.arange(EXPERTS, dtype=jnp.int32)
    onehot = (flat_routes[:, None] == expert_ids[None, :]).astype(jnp.int32)
    before = jnp.cumsum(onehot, axis=0) - onehot
    ranks = lax.optimization_barrier(jnp.sum(before * onehot, axis=1))
    slot_ids = (flat_routes * CAP + ranks).reshape(block_routes.shape)
    slot_range = jnp.arange(EXPERTS * CAP, dtype=jnp.int32)
    matches = slot_ids[None, :, :] == slot_range[:, None, None]
    dispatch = jnp.any(matches, axis=-1).astype(jnp.bfloat16)
    combine = lax.optimization_barrier(jnp.sum(jnp.where(matches, block_gates[None, :, :], 0.0), axis=-1)).T.astype(jnp.float32)
    return (dispatch, combine)

def attend_request(operands):
    request_q, cache_k, cache_v, fresh_k, fresh_v, length = operands
    all_keys = jnp.concatenate([cache_k, fresh_k], axis=0).reshape(CACHE + POS, HEADS, HD)
    all_values = jnp.concatenate([cache_v, fresh_v], axis=0).reshape(CACHE + POS, HEADS, HD)
    request_q = request_q.reshape(POS, HEADS, HD)
    scores = jnp.einsum('phd,jhd->hpj', request_q.astype(jnp.float32), all_keys.astype(jnp.float32)) * HD ** (-0.5)
    key_pos = jnp.arange(CACHE + POS, dtype=jnp.int32)
    query_pos = jnp.arange(POS, dtype=jnp.int32)
    live = jnp.where(key_pos[None, :] < CACHE, key_pos[None, :] < length, key_pos[None, :] - CACHE <= query_pos[:, None])
    scores = jnp.where(live[None, :, :], scores, -1e+30)
    top = lax.optimization_barrier(jnp.max(scores, axis=-1, keepdims=True))
    expo = jnp.exp(scores - top)
    weights = (expo / lax.optimization_barrier(jnp.sum(expo, axis=-1, keepdims=True))).astype(jnp.bfloat16)
    attended = jnp.einsum('hpj,jhd->phd', weights.astype(jnp.float32), all_values.astype(jnp.float32))
    return attended.astype(jnp.bfloat16).reshape(POS, HEADS * HD)

def expert_apply(operands):
    rows, w_gate, w_up, w_down = operands
    gated = jnp.dot(rows, w_gate, preferred_element_type=jnp.float32)
    upward = jnp.dot(rows, w_up, preferred_element_type=jnp.float32)
    activation = (jax.nn.silu(gated) * upward).astype(jnp.bfloat16)
    return jnp.dot(activation, w_down, preferred_element_type=jnp.float32)

def reference(queries, new_keys, new_values, cache_keys, cache_values, cache_lengths, hidden_in, out_weight, norm_gain, routes, route_gates, gate_weight, up_weight, down_weight):
    q_req = queries.reshape(REQUESTS, POS, HEADS * HD)
    k_req = new_keys.reshape(REQUESTS, POS, HEADS * HD)
    v_req = new_values.reshape(REQUESTS, POS, HEADS * HD)
    attended = lax.map(attend_request, (q_req, cache_keys, cache_values, k_req, v_req, cache_lengths))
    attended = attended.reshape(TOKENS, HEADS * HD)
    summed = jnp.dot(attended, out_weight, preferred_element_type=jnp.float32) + hidden_in.astype(jnp.float32)
    mean_square = lax.optimization_barrier(jnp.mean(summed * summed, axis=-1, keepdims=True))
    normed = (summed * lax.rsqrt(mean_square + 1e-06) * norm_gain[None, :]).astype(jnp.bfloat16)
    blocks = TOKENS // TOK_DEV
    dispatch, combine = jax.vmap(slot_tables)(routes.reshape(blocks, TOK_DEV, TOPK), route_gates.reshape(blocks, TOK_DEV, TOPK))
    outbound = jnp.einsum('bst,btd->bsd', dispatch.astype(jnp.float32), normed.reshape(blocks, TOK_DEV, D).astype(jnp.float32)).astype(jnp.bfloat16)
    per_expert = outbound.reshape(blocks, EXPERTS, CAP, D).transpose(1, 0, 2, 3).reshape(EXPERTS, blocks * CAP, D)
    results = lax.map(expert_apply, (per_expert, gate_weight, up_weight, down_weight))
    results = results.reshape(EXPERTS, blocks, CAP, D).transpose(1, 0, 2, 3).reshape(blocks, EXPERTS * CAP, D)
    expert_sum = jnp.einsum('bts,bsd->btd', combine, results, precision=lax.Precision.HIGHEST).reshape(TOKENS, D)
    return (summed + expert_sum).astype(jnp.bfloat16)
```

```python
import jax
import jax.numpy as jnp
from jax import lax
from jax.sharding import PartitionSpec as P

HD = 128
EXPERTS = 64
POS = 5
CACHE = 384
CAP = 3


def slot_tables(local_routes, local_gates):
    flat_routes = local_routes.reshape(-1)
    expert_ids = jnp.arange(EXPERTS, dtype=jnp.int32)
    onehot = (flat_routes[:, None] == expert_ids[None, :]).astype(jnp.int32)
    before = jnp.cumsum(onehot, axis=0) - onehot
    ranks = jnp.sum(before * onehot, axis=1)
    slot_ids = (flat_routes * CAP + ranks).reshape(local_routes.shape)
    slot_range = jnp.arange(EXPERTS * CAP, dtype=jnp.int32)
    matches = slot_ids[None, :, :] == slot_range[:, None, None]
    dispatch = jnp.any(matches, axis=-1).astype(jnp.bfloat16)
    combine = jnp.sum(jnp.where(matches, local_gates[None, :, :], 0.0), axis=-1).T
    return (dispatch, combine)


def attend_local(queries, new_keys, new_values, cache_keys, cache_values, cache_lengths):
    req_count = cache_keys.shape[0]
    head_count = queries.shape[1] // HD
    all_keys = jnp.concatenate([cache_keys, new_keys.reshape(req_count, POS, -1)], axis=1).reshape(
        req_count, CACHE + POS, head_count, HD
    )
    all_values = jnp.concatenate(
        [cache_values, new_values.reshape(req_count, POS, -1)], axis=1
    ).reshape(req_count, CACHE + POS, head_count, HD)
    local_q = queries.reshape(req_count, POS, head_count, HD)
    scores = jnp.einsum(
        "rphd,rjhd->rhpj", local_q, all_keys, preferred_element_type=jnp.float32
    ) * HD ** (-0.5)
    key_pos = jnp.arange(CACHE + POS, dtype=jnp.int32)
    query_pos = jnp.arange(POS, dtype=jnp.int32)
    cache_live = key_pos[None, None, :] < cache_lengths[:, None, None]
    fresh_live = key_pos[None, None, :] - CACHE <= query_pos[None, :, None]
    live = jnp.where(key_pos[None, None, :] < CACHE, cache_live, fresh_live)
    scores = jnp.where(live[:, None, :, :], scores, -1e30)
    top = jnp.max(scores, axis=-1, keepdims=True)
    expo = jnp.exp(scores - top)
    weights = (expo / jnp.sum(expo, axis=-1, keepdims=True)).astype(jnp.bfloat16)
    attended = jnp.einsum(
        "rhpj,rjhd->rphd", weights, all_values, preferred_element_type=jnp.float32
    )
    return attended.astype(jnp.bfloat16).reshape(req_count * POS, head_count * HD)


def expert_apply(slot_rows, gate_weight, up_weight, down_weight):
    gated = jnp.einsum("secd,edf->secf", slot_rows, gate_weight, preferred_element_type=jnp.float32)
    upward = jnp.einsum("secd,edf->secf", slot_rows, up_weight, preferred_element_type=jnp.float32)
    activation = (jax.nn.silu(gated) * upward).astype(jnp.bfloat16)
    return jnp.einsum("secf,efd->secd", activation, down_weight, preferred_element_type=jnp.float32)


def scatter_sum(value, tp_count):
    rows, width = value.shape
    pieces = value.reshape(rows, tp_count, width // tp_count).transpose(1, 0, 2)
    pieces = lax.all_to_all(pieces, "tp", split_axis=0, concat_axis=0, tiled=True)
    return jnp.sum(pieces.astype(jnp.float32), axis=0)


def gather_cols(value, tp_count):
    rows, columns = value.shape
    pieces = jnp.broadcast_to(value[None], (tp_count, rows, columns))
    pieces = lax.all_to_all(pieces, "tp", split_axis=0, concat_axis=0, tiled=True)
    return pieces.transpose(1, 0, 2).reshape(rows, tp_count * columns)


def local(
    queries,
    new_keys,
    new_values,
    cache_keys,
    cache_values,
    cache_lengths,
    hidden_in,
    out_weight,
    norm_gain,
    routes,
    route_gates,
    gate_weight,
    up_weight,
    down_weight,
):
    attended = attend_local(queries, new_keys, new_values, cache_keys, cache_values, cache_lengths)
    partial_value = jnp.dot(attended, out_weight, preferred_element_type=jnp.float32)
    model_width = partial_value.shape[1]
    tp_count = lax.axis_size("tp")
    columns = model_width // tp_count
    offset = lax.axis_index("tp") * columns
    holders = lax.axis_size("req")
    dispatch, combine = slot_tables(routes, route_gates)
    hidden_cols = lax.dynamic_slice_in_dim(hidden_in, offset, columns, 1).astype(jnp.float32)
    summed_cols = scatter_sum(partial_value, tp_count) + hidden_cols
    summed = gather_cols(summed_cols, tp_count)
    mean_square = jnp.mean(summed * summed, axis=-1, keepdims=True)
    normed = (summed * lax.rsqrt(mean_square + 1e-06) * norm_gain[None, :]).astype(jnp.bfloat16)
    outbound = jnp.dot(dispatch, normed, preferred_element_type=jnp.float32).astype(jnp.bfloat16)
    outbound = outbound.reshape(holders, -1, CAP, model_width)
    produced = expert_apply(
        lax.all_to_all(outbound, "req", split_axis=0, concat_axis=0, tiled=True),
        gate_weight,
        up_weight,
        down_weight,
    )
    returned = lax.all_to_all(
        produced.astype(jnp.bfloat16), "req", split_axis=0, concat_axis=0, tiled=True
    ).astype(produced.dtype)
    expert_sum = jnp.dot(
        combine,
        returned.reshape(-1, model_width),
        precision=lax.Precision.HIGHEST,
        preferred_element_type=jnp.float32,
    )
    expert_cols = scatter_sum(expert_sum.astype(jnp.bfloat16), tp_count)
    return (summed_cols + expert_cols).astype(jnp.bfloat16)


def solution(mesh):
    in_specs = (
        P("req", "tp"),
        P("req", "tp"),
        P("req", "tp"),
        P("req", None, "tp"),
        P("req", None, "tp"),
        P("req"),
        P("req", None),
        P("tp", None),
        P(),
        P("req", None),
        P("req", None),
        P("req", None, "tp"),
        P("req", None, "tp"),
        P("req", "tp", None),
    )
    out_specs = P("req", "tp")
    return jax.shard_map(local, mesh=mesh, in_specs=in_specs, out_specs=out_specs, check_vma=False)
```

```python
import jax
import jax.numpy as jnp
from jax import lax
from jax.experimental import pallas as pl
from jax.experimental.pallas import tpu as pltpu
from jax.sharding import PartitionSpec as P

HD = 128
EXPERTS = 64
POS = 5
CACHE = 384
CAP = 3


def slot_tables(local_routes, local_gates):
    flat_routes = local_routes.reshape(-1)
    expert_ids = jnp.arange(EXPERTS, dtype=jnp.int32)
    onehot = (flat_routes[:, None] == expert_ids[None, :]).astype(jnp.int32)
    before = jnp.cumsum(onehot, axis=0) - onehot
    ranks = jnp.sum(before * onehot, axis=1)
    slot_ids = (flat_routes * CAP + ranks).reshape(local_routes.shape)
    slot_range = jnp.arange(EXPERTS * CAP, dtype=jnp.int32)
    matches = slot_ids[None, :, :] == slot_range[:, None, None]
    dispatch = jnp.any(matches, axis=-1).astype(jnp.bfloat16)
    combine = jnp.sum(jnp.where(matches, local_gates[None, :, :], 0.0), axis=-1).T
    return (dispatch, combine)


def attend_project(queries, new_keys, new_values, cache_keys, cache_values, cache_lengths, out_weight, tp_count):
    req_count, cache_len, width = cache_keys.shape
    tokens = queries.shape[0]
    model_width = out_weight.shape[1]
    columns = model_width // tp_count
    head_count = width // HD
    flat_k = cache_keys.reshape(req_count * cache_len, width)
    flat_v = cache_values.reshape(req_count * cache_len, width)

    def kernel(len_ref, q_ref, nk_ref, nv_ref, ck_ref, cv_ref, ow_ref, out_ref):
        row = lax.broadcasted_iota(jnp.int32, (tokens, 1), 0)
        lo = jnp.zeros((tokens, 1), jnp.int32)
        hi = jnp.zeros((tokens, 1), jnp.int32)
        first = jnp.zeros((tokens, 1), jnp.int32)
        for r in range(req_count):
            mine = (row >= r * POS) & (row < (r + 1) * POS)
            lo = jnp.where(mine, r * cache_len, lo)
            hi = jnp.where(mine, r * cache_len + len_ref[r], hi)
            first = jnp.where(mine, r * POS, first)
        key_at = lax.broadcasted_iota(jnp.int32, (tokens, req_count * cache_len), 1)
        live_c = (key_at >= lo) & (key_at < hi)
        fresh_at = lax.broadcasted_iota(jnp.int32, (tokens, tokens), 1)
        live_n = (fresh_at >= first) & (fresh_at <= row)
        dims = (((1,), (1,)), ((), ()))
        heads = []
        for h in range(head_count):
            cols = slice(h * HD, (h + 1) * HD)
            q = q_ref[:, cols]
            sc = lax.dot_general(q, ck_ref[:, cols], dims, preferred_element_type=jnp.float32) * HD ** (-0.5)
            sn = lax.dot_general(q, nk_ref[:, cols], dims, preferred_element_type=jnp.float32) * HD ** (-0.5)
            sc = jnp.where(live_c, sc, -1e30)
            sn = jnp.where(live_n, sn, -1e30)
            top = jnp.maximum(jnp.max(sc, axis=1, keepdims=True), jnp.max(sn, axis=1, keepdims=True))
            ec = jnp.exp(sc - top)
            en = jnp.exp(sn - top)
            total = jnp.sum(ec, axis=1, keepdims=True) + jnp.sum(en, axis=1, keepdims=True)
            wc = (ec / total).astype(jnp.bfloat16)
            wn = (en / total).astype(jnp.bfloat16)
            att = jnp.dot(wc, cv_ref[:, cols], preferred_element_type=jnp.float32)
            att = att + jnp.dot(wn, nv_ref[:, cols], preferred_element_type=jnp.float32)
            heads.append(att.astype(jnp.bfloat16))
        attended = jnp.concatenate(heads, axis=1)
        partial = jnp.dot(attended, ow_ref[...], preferred_element_type=jnp.float32)
        for k in range(tp_count):
            out_ref[k] = partial[:, k * columns:(k + 1) * columns]

    vmem = pl.BlockSpec(memory_space=pltpu.VMEM)
    return pl.pallas_call(
        kernel,
        out_shape=jax.ShapeDtypeStruct((tp_count, tokens, columns), jnp.float32),
        in_specs=[pl.BlockSpec(memory_space=pltpu.SMEM)] + [vmem] * 6,
        out_specs=vmem,
    )(cache_lengths, queries, new_keys, new_values, flat_k, flat_v, out_weight)


def expert_apply(slot_rows, gate_weight, up_weight, down_weight):
    gated = jnp.einsum("secd,edf->secf", slot_rows, gate_weight, preferred_element_type=jnp.float32)
    upward = jnp.einsum("secd,edf->secf", slot_rows, up_weight, preferred_element_type=jnp.float32)
    activation = (jax.nn.silu(gated) * upward).astype(jnp.bfloat16)
    return jnp.einsum("secf,efd->secd", activation, down_weight, preferred_element_type=jnp.float32)


def scatter_sum(value, tp_count):
    rows, width = value.shape
    pieces = value.reshape(rows, tp_count, width // tp_count).transpose(1, 0, 2)
    pieces = lax.all_to_all(pieces, "tp", split_axis=0, concat_axis=0, tiled=True)
    return jnp.sum(pieces.astype(jnp.float32), axis=0)


def gather_cols(value, tp_count):
    rows, columns = value.shape
    pieces = jnp.broadcast_to(value[None], (tp_count, rows, columns))
    pieces = lax.all_to_all(pieces, "tp", split_axis=0, concat_axis=0, tiled=True)
    return pieces.transpose(1, 0, 2).reshape(rows, tp_count * columns)


def local(
    queries,
    new_keys,
    new_values,
    cache_keys,
    cache_values,
    cache_lengths,
    hidden_in,
    out_weight,
    norm_gain,
    routes,
    route_gates,
    gate_weight,
    up_weight,
    down_weight,
):
    model_width = out_weight.shape[1]
    tp_count = lax.axis_size("tp")
    pieces = attend_project(
        queries, new_keys, new_values, cache_keys, cache_values, cache_lengths, out_weight, tp_count
    )
    columns = model_width // tp_count
    offset = lax.axis_index("tp") * columns
    holders = lax.axis_size("req")
    dispatch, combine = slot_tables(routes, route_gates)
    hidden_cols = lax.dynamic_slice_in_dim(hidden_in, offset, columns, 1).astype(jnp.float32)
    pieces = lax.all_to_all(pieces, "tp", split_axis=0, concat_axis=0, tiled=True)
    summed_cols = jnp.sum(pieces, axis=0) + hidden_cols
    summed = gather_cols(summed_cols, tp_count)
    mean_square = jnp.mean(summed * summed, axis=-1, keepdims=True)
    normed = (summed * lax.rsqrt(mean_square + 1e-06) * norm_gain[None, :]).astype(jnp.bfloat16)
    outbound = jnp.dot(dispatch, normed, preferred_element_type=jnp.float32).astype(jnp.bfloat16)
    outbound = outbound.reshape(holders, -1, CAP, model_width)
    produced = expert_apply(
        lax.all_to_all(outbound, "req", split_axis=0, concat_axis=0, tiled=True),
        gate_weight,
        up_weight,
        down_weight,
    )
    returned = lax.all_to_all(
        produced.astype(jnp.bfloat16), "req", split_axis=0, concat_axis=0, tiled=True
    ).astype(produced.dtype)
    expert_sum = jnp.dot(
        combine,
        returned.reshape(-1, model_width),
        precision=lax.Precision.HIGHEST,
        preferred_element_type=jnp.float32,
    )
    expert_cols = scatter_sum(expert_sum.astype(jnp.bfloat16), tp_count)
    return (summed_cols + expert_cols).astype(jnp.bfloat16)


def solution(mesh):
    in_specs = (
        P("req", "tp"),
        P("req", "tp"),
        P("req", "tp"),
        P("req", None, "tp"),
        P("req", None, "tp"),
        P("req"),
        P("req", None),
        P("tp", None),
        P(),
        P("req", None),
        P("req", None),
        P("req", None, "tp"),
        P("req", None, "tp"),
        P("req", "tp", None),
    )
    out_specs = P("req", "tp")
    return jax.shard_map(local, mesh=mesh, in_specs=in_specs, out_specs=out_specs, check_vma=False)
```

```python
import jax
import jax.numpy as jnp
from jax import lax
from jax.experimental import pallas as pl
from jax.experimental.pallas import tpu as pltpu
from jax.sharding import PartitionSpec as P

HD = 128
EXPERTS = 64
POS = 5
CACHE = 384
CAP = 3


def slot_tables(local_routes, local_gates):
    flat_routes = local_routes.reshape(-1)
    expert_ids = jnp.arange(EXPERTS, dtype=jnp.int32)
    onehot = (flat_routes[:, None] == expert_ids[None, :]).astype(jnp.int32)
    before = jnp.cumsum(onehot, axis=0) - onehot
    ranks = jnp.sum(before * onehot, axis=1)
    slot_ids = (flat_routes * CAP + ranks).reshape(local_routes.shape)
    slot_range = jnp.arange(EXPERTS * CAP, dtype=jnp.int32)
    matches = slot_ids[None, :, :] == slot_range[:, None, None]
    dispatch = jnp.any(matches, axis=-1).astype(jnp.bfloat16)
    combine = jnp.sum(jnp.where(matches, local_gates[None, :, :], 0.0), axis=-1).T
    return (dispatch, combine)


def attend_project(queries, new_keys, new_values, cache_keys, cache_values, cache_lengths, out_weight, tp_count):
    req_count, cache_len, width = cache_keys.shape
    tokens = queries.shape[0]
    model_width = out_weight.shape[1]
    columns = model_width // tp_count
    head_count = width // HD
    flat_k = cache_keys.reshape(req_count * cache_len, width)
    flat_v = cache_values.reshape(req_count * cache_len, width)

    def kernel(len_ref, q_ref, nk_ref, nv_ref, ck_ref, cv_ref, ow_ref, out_ref):
        row = lax.broadcasted_iota(jnp.int32, (tokens, 1), 0)
        lo = jnp.zeros((tokens, 1), jnp.int32)
        hi = jnp.zeros((tokens, 1), jnp.int32)
        first = jnp.zeros((tokens, 1), jnp.int32)
        for r in range(req_count):
            mine = (row >= r * POS) & (row < (r + 1) * POS)
            lo = jnp.where(mine, r * cache_len, lo)
            hi = jnp.where(mine, r * cache_len + len_ref[r], hi)
            first = jnp.where(mine, r * POS, first)
        key_at = lax.broadcasted_iota(jnp.int32, (tokens, req_count * cache_len), 1)
        live_c = (key_at >= lo) & (key_at < hi)
        fresh_at = lax.broadcasted_iota(jnp.int32, (tokens, tokens), 1)
        live_n = (fresh_at >= first) & (fresh_at <= row)
        dims = (((1,), (1,)), ((), ()))
        heads = []
        for h in range(head_count):
            cols = slice(h * HD, (h + 1) * HD)
            q = q_ref[:, cols]
            sc = lax.dot_general(q, ck_ref[:, cols], dims, preferred_element_type=jnp.float32) * HD ** (-0.5)
            sn = lax.dot_general(q, nk_ref[:, cols], dims, preferred_element_type=jnp.float32) * HD ** (-0.5)
            sc = jnp.where(live_c, sc, -1e30)
            sn = jnp.where(live_n, sn, -1e30)
            top = jnp.maximum(jnp.max(sc, axis=1, keepdims=True), jnp.max(sn, axis=1, keepdims=True))
            ec = jnp.exp(sc - top)
            en = jnp.exp(sn - top)
            total = jnp.sum(ec, axis=1, keepdims=True) + jnp.sum(en, axis=1, keepdims=True)
            wc = (ec / total).astype(jnp.bfloat16)
            wn = (en / total).astype(jnp.bfloat16)
            att = jnp.dot(wc, cv_ref[:, cols], preferred_element_type=jnp.float32)
            att = att + jnp.dot(wn, nv_ref[:, cols], preferred_element_type=jnp.float32)
            heads.append(att.astype(jnp.bfloat16))
        attended = jnp.concatenate(heads, axis=1)
        partial = jnp.dot(attended, ow_ref[...], preferred_element_type=jnp.float32)
        for k in range(tp_count):
            out_ref[k] = partial[:, k * columns:(k + 1) * columns]

    vmem = pl.BlockSpec(memory_space=pltpu.VMEM)
    return pl.pallas_call(
        kernel,
        out_shape=jax.ShapeDtypeStruct((tp_count, tokens, columns), jnp.float32),
        in_specs=[pl.BlockSpec(memory_space=pltpu.SMEM)] + [vmem] * 6,
        out_specs=vmem,
    )(cache_lengths, queries, new_keys, new_values, flat_k, flat_v, out_weight)


def expert_apply(slot_rows, gate_weight, up_weight, down_weight):
    gated = jnp.einsum("secd,edf->secf", slot_rows, gate_weight, preferred_element_type=jnp.float32)
    upward = jnp.einsum("secd,edf->secf", slot_rows, up_weight, preferred_element_type=jnp.float32)
    activation = (jax.nn.silu(gated) * upward).astype(jnp.bfloat16)
    return jnp.einsum("secf,efd->secd", activation, down_weight, preferred_element_type=jnp.float32)


def scatter_sum(value, tp_count):
    rows, width = value.shape
    pieces = value.reshape(rows, tp_count, width // tp_count).transpose(1, 0, 2)
    pieces = lax.all_to_all(pieces, "tp", split_axis=0, concat_axis=0, tiled=True)
    return jnp.sum(pieces.astype(jnp.float32), axis=0)


def gather_cols(value, tp_count):
    rows, columns = value.shape
    pieces = jnp.broadcast_to(value[None], (tp_count, rows, columns))
    pieces = lax.all_to_all(pieces, "tp", split_axis=0, concat_axis=0, tiled=True)
    return pieces.transpose(1, 0, 2).reshape(rows, tp_count * columns)


def local(
    queries,
    new_keys,
    new_values,
    cache_keys,
    cache_values,
    cache_lengths,
    hidden_in,
    out_weight,
    norm_gain,
    routes,
    route_gates,
    gate_weight,
    up_weight,
    down_weight,
):
    model_width = out_weight.shape[1]
    tp_count = lax.axis_size("tp")
    pieces = attend_project(
        queries, new_keys, new_values, cache_keys, cache_values, cache_lengths, out_weight, tp_count
    )
    columns = model_width // tp_count
    offset = lax.axis_index("tp") * columns
    holders = lax.axis_size("req")
    dispatch, combine = slot_tables(routes, route_gates)
    hidden_cols = lax.dynamic_slice_in_dim(hidden_in, offset, columns, 1).astype(jnp.float32)
    pieces = lax.all_to_all(pieces, "tp", split_axis=0, concat_axis=0, tiled=True)
    summed_cols = jnp.sum(pieces, axis=0) + hidden_cols
    summed = gather_cols(summed_cols, tp_count)
    mean_square = jnp.mean(summed * summed, axis=-1, keepdims=True)
    normed = (summed * lax.rsqrt(mean_square + 1e-06) * norm_gain[None, :]).astype(jnp.bfloat16)
    outbound = jnp.dot(dispatch, normed, preferred_element_type=jnp.float32).astype(jnp.bfloat16)
    packed = (holders, CAP * model_width // 128, 128)
    outbound = outbound.reshape(packed)
    arrived = lax.all_to_all(outbound, "req", split_axis=0, concat_axis=0, tiled=True)
    produced = expert_apply(
        arrived.reshape(holders, 1, CAP, model_width),
        gate_weight,
        up_weight,
        down_weight,
    )
    returned = lax.all_to_all(
        produced.astype(jnp.bfloat16).reshape(packed), "req", split_axis=0, concat_axis=0, tiled=True
    ).astype(produced.dtype)
    expert_sum = jnp.dot(
        combine,
        returned.reshape(-1, model_width),
        precision=lax.Precision.HIGHEST,
        preferred_element_type=jnp.float32,
    )
    expert_cols = scatter_sum(expert_sum.astype(jnp.bfloat16), tp_count)
    return (summed_cols + expert_cols).astype(jnp.bfloat16)


def solution(mesh):
    in_specs = (
        P("req", "tp"),
        P("req", "tp"),
        P("req", "tp"),
        P("req", None, "tp"),
        P("req", None, "tp"),
        P("req"),
        P("req", None),
        P("tp", None),
        P(),
        P("req", None),
        P("req", None),
        P("req", None, "tp"),
        P("req", None, "tp"),
        P("req", "tp", None),
    )
    out_specs = P("req", "tp")
    return jax.shard_map(local, mesh=mesh, in_specs=in_specs, out_specs=out_specs, check_vma=False)
```

```python
import jax
import jax.numpy as jnp
from jax import lax
from jax.experimental import pallas as pl
from jax.experimental.pallas import tpu as pltpu
from jax.sharding import PartitionSpec as P

HD = 128
EXPERTS = 64
POS = 5
CACHE = 384
CAP = 3


def slot_tables(local_routes, local_gates):
    flat_routes = local_routes.reshape(-1)
    expert_ids = jnp.arange(EXPERTS, dtype=jnp.int32)
    onehot = (flat_routes[:, None] == expert_ids[None, :]).astype(jnp.int32)
    before = jnp.cumsum(onehot, axis=0) - onehot
    ranks = jnp.sum(before * onehot, axis=1)
    slot_ids = (flat_routes * CAP + ranks).reshape(local_routes.shape)
    slot_range = jnp.arange(EXPERTS * CAP, dtype=jnp.int32)
    matches = slot_ids[None, :, :] == slot_range[:, None, None]
    dispatch = jnp.any(matches, axis=-1).astype(jnp.bfloat16)
    combine = jnp.sum(jnp.where(matches, local_gates[None, :, :], 0.0), axis=-1).T
    return (dispatch, combine)


def attend_project(queries, new_keys, new_values, cache_keys, cache_values, cache_lengths, out_weight, tp_count):
    req_count, cache_len, width = cache_keys.shape
    tokens = queries.shape[0]
    model_width = out_weight.shape[1]
    columns = model_width // tp_count
    head_count = width // HD
    flat_k = cache_keys.reshape(req_count * cache_len, width)
    flat_v = cache_values.reshape(req_count * cache_len, width)

    def kernel(len_ref, q_ref, nk_ref, nv_ref, ck_ref, cv_ref, ow_ref, out_ref):
        row = lax.broadcasted_iota(jnp.int32, (tokens, 1), 0)
        lo = jnp.zeros((tokens, 1), jnp.int32)
        hi = jnp.zeros((tokens, 1), jnp.int32)
        first = jnp.zeros((tokens, 1), jnp.int32)
        for r in range(req_count):
            mine = (row >= r * POS) & (row < (r + 1) * POS)
            lo = jnp.where(mine, r * cache_len, lo)
            hi = jnp.where(mine, r * cache_len + len_ref[r], hi)
            first = jnp.where(mine, r * POS, first)
        key_at = lax.broadcasted_iota(jnp.int32, (tokens, req_count * cache_len), 1)
        live_c = (key_at >= lo) & (key_at < hi)
        fresh_at = lax.broadcasted_iota(jnp.int32, (tokens, tokens), 1)
        live_n = (fresh_at >= first) & (fresh_at <= row)
        dims = (((1,), (1,)), ((), ()))
        heads = []
        for h in range(head_count):
            cols = slice(h * HD, (h + 1) * HD)
            q = q_ref[:, cols]
            sc = lax.dot_general(q, ck_ref[:, cols], dims, preferred_element_type=jnp.float32) * HD ** (-0.5)
            sn = lax.dot_general(q, nk_ref[:, cols], dims, preferred_element_type=jnp.float32) * HD ** (-0.5)
            sc = jnp.where(live_c, sc, -1e30)
            sn = jnp.where(live_n, sn, -1e30)
            top = jnp.maximum(jnp.max(sc, axis=1, keepdims=True), jnp.max(sn, axis=1, keepdims=True))
            ec = jnp.exp(sc - top)
            en = jnp.exp(sn - top)
            total = jnp.sum(ec, axis=1, keepdims=True) + jnp.sum(en, axis=1, keepdims=True)
            wc = (ec / total).astype(jnp.bfloat16)
            wn = (en / total).astype(jnp.bfloat16)
            att = jnp.dot(wc, cv_ref[:, cols], preferred_element_type=jnp.float32)
            att = att + jnp.dot(wn, nv_ref[:, cols], preferred_element_type=jnp.float32)
            heads.append(att.astype(jnp.bfloat16))
        attended = jnp.concatenate(heads, axis=1)
        partial = jnp.dot(attended, ow_ref[...], preferred_element_type=jnp.float32)
        half = columns // 2
        for k in range(tp_count):
            out_ref[k, 0:tokens, :] = partial[:, k * columns:k * columns + half]
            out_ref[k, tokens:2 * tokens, :] = partial[:, k * columns + half:(k + 1) * columns]

    vmem = pl.BlockSpec(memory_space=pltpu.VMEM)
    return pl.pallas_call(
        kernel,
        out_shape=jax.ShapeDtypeStruct((tp_count, 2 * tokens, columns // 2), jnp.float32),
        in_specs=[pl.BlockSpec(memory_space=pltpu.SMEM)] + [vmem] * 6,
        out_specs=vmem,
    )(cache_lengths, queries, new_keys, new_values, flat_k, flat_v, out_weight)


def expert_apply(slot_rows, gate_weight, up_weight, down_weight):
    gated = jnp.einsum("secd,edf->secf", slot_rows, gate_weight, preferred_element_type=jnp.float32)
    upward = jnp.einsum("secd,edf->secf", slot_rows, up_weight, preferred_element_type=jnp.float32)
    activation = (jax.nn.silu(gated) * upward).astype(jnp.bfloat16)
    return jnp.einsum("secf,efd->secd", activation, down_weight, preferred_element_type=jnp.float32)


def stack_halves(value):
    half = value.shape[1] // 2
    return jnp.concatenate([value[:, :half], value[:, half:]], axis=0)


def unstack_halves(value):
    rows = value.shape[0] // 2
    return jnp.concatenate([value[:rows], value[rows:]], axis=1)


def scatter_sum(value, tp_count):
    rows, width = value.shape
    pieces = value.reshape(rows, tp_count, 2, width // tp_count // 2).transpose(1, 2, 0, 3)
    pieces = pieces.reshape(tp_count, 2 * rows, width // tp_count // 2)
    pieces = lax.all_to_all(pieces, "tp", split_axis=0, concat_axis=0, tiled=True)
    return unstack_halves(jnp.sum(pieces.astype(jnp.float32), axis=0))


def gather_cols(value, tp_count):
    rows, columns = value.shape
    stacked = stack_halves(value)
    pieces = jnp.broadcast_to(stacked[None], (tp_count,) + stacked.shape)
    pieces = lax.all_to_all(pieces, "tp", split_axis=0, concat_axis=0, tiled=True)
    pieces = pieces.reshape(tp_count, 2, rows, columns // 2).transpose(2, 0, 1, 3)
    return pieces.reshape(rows, tp_count * columns)


def local(
    queries,
    new_keys,
    new_values,
    cache_keys,
    cache_values,
    cache_lengths,
    hidden_in,
    out_weight,
    norm_gain,
    routes,
    route_gates,
    gate_weight,
    up_weight,
    down_weight,
):
    model_width = out_weight.shape[1]
    tp_count = lax.axis_size("tp")
    pieces = attend_project(
        queries, new_keys, new_values, cache_keys, cache_values, cache_lengths, out_weight, tp_count
    )
    columns = model_width // tp_count
    offset = lax.axis_index("tp") * columns
    holders = lax.axis_size("req")
    dispatch, combine = slot_tables(routes, route_gates)
    hidden_cols = lax.dynamic_slice_in_dim(hidden_in, offset, columns, 1).astype(jnp.float32)
    pieces = lax.all_to_all(pieces, "tp", split_axis=0, concat_axis=0, tiled=True)
    summed_cols = unstack_halves(jnp.sum(pieces, axis=0)) + hidden_cols
    summed = gather_cols(summed_cols, tp_count)
    mean_square = jnp.mean(summed * summed, axis=-1, keepdims=True)
    normed = (summed * lax.rsqrt(mean_square + 1e-06) * norm_gain[None, :]).astype(jnp.bfloat16)
    outbound = jnp.dot(dispatch, normed, preferred_element_type=jnp.float32).astype(jnp.bfloat16)
    packed = (holders, CAP * model_width // 128, 128)
    outbound = outbound.reshape(packed)
    arrived = lax.all_to_all(outbound, "req", split_axis=0, concat_axis=0, tiled=True)
    produced = expert_apply(
        arrived.reshape(holders, 1, CAP, model_width),
        gate_weight,
        up_weight,
        down_weight,
    )
    returned = lax.all_to_all(
        produced.astype(jnp.bfloat16).reshape(packed), "req", split_axis=0, concat_axis=0, tiled=True
    ).astype(produced.dtype)
    expert_sum = jnp.dot(
        combine,
        returned.reshape(-1, model_width),
        precision=lax.Precision.HIGHEST,
        preferred_element_type=jnp.float32,
    )
    expert_cols = scatter_sum(expert_sum.astype(jnp.bfloat16), tp_count)
    return (summed_cols + expert_cols).astype(jnp.bfloat16)


def solution(mesh):
    in_specs = (
        P("req", "tp"),
        P("req", "tp"),
        P("req", "tp"),
        P("req", None, "tp"),
        P("req", None, "tp"),
        P("req"),
        P("req", None),
        P("tp", None),
        P(),
        P("req", None),
        P("req", None),
        P("req", None, "tp"),
        P("req", None, "tp"),
        P("req", "tp", None),
    )
    out_specs = P("req", "tp")
    return jax.shard_map(local, mesh=mesh, in_specs=in_specs, out_specs=out_specs, check_vma=False)
```

```python
import jax
import jax.numpy as jnp
from jax import lax
from jax.experimental import pallas as pl
from jax.experimental.pallas import tpu as pltpu
from jax.sharding import PartitionSpec as P

HD = 128
EXPERTS = 64
POS = 5
CACHE = 384
CAP = 3


def slot_tables(local_routes, local_gates):
    flat_routes = local_routes.reshape(-1)
    expert_ids = jnp.arange(EXPERTS, dtype=jnp.int32)
    onehot = (flat_routes[:, None] == expert_ids[None, :]).astype(jnp.int32)
    before = jnp.cumsum(onehot, axis=0) - onehot
    ranks = jnp.sum(before * onehot, axis=1)
    slot_ids = (flat_routes * CAP + ranks).reshape(local_routes.shape)
    slot_range = jnp.arange(EXPERTS * CAP, dtype=jnp.int32)
    matches = slot_ids[None, :, :] == slot_range[:, None, None]
    dispatch = jnp.any(matches, axis=-1).astype(jnp.bfloat16)
    combine = jnp.sum(jnp.where(matches, local_gates[None, :, :], 0.0), axis=-1).T
    return (dispatch, combine)


def attend_project(queries, new_keys, new_values, cache_keys, cache_values, cache_lengths, out_weight, tp_count):
    req_count, cache_len, width = cache_keys.shape
    tokens = queries.shape[0]
    model_width = out_weight.shape[1]
    columns = model_width // tp_count
    head_count = width // HD
    flat_k = cache_keys.reshape(req_count * cache_len, width)
    flat_v = cache_values.reshape(req_count * cache_len, width)

    def kernel(len_ref, q_ref, nk_ref, nv_ref, ck_ref, cv_ref, ow_ref, out_ref):
        row = lax.broadcasted_iota(jnp.int32, (tokens, 1), 0)
        lo = jnp.zeros((tokens, 1), jnp.int32)
        hi = jnp.zeros((tokens, 1), jnp.int32)
        first = jnp.zeros((tokens, 1), jnp.int32)
        for r in range(req_count):
            mine = (row >= r * POS) & (row < (r + 1) * POS)
            lo = jnp.where(mine, r * cache_len, lo)
            hi = jnp.where(mine, r * cache_len + len_ref[r], hi)
            first = jnp.where(mine, r * POS, first)
        key_at = lax.broadcasted_iota(jnp.int32, (tokens, req_count * cache_len), 1)
        live_c = (key_at >= lo) & (key_at < hi)
        fresh_at = lax.broadcasted_iota(jnp.int32, (tokens, tokens), 1)
        live_n = (fresh_at >= first) & (fresh_at <= row)
        dims = (((1,), (1,)), ((), ()))
        heads = []
        for h in range(head_count):
            cols = slice(h * HD, (h + 1) * HD)
            q = q_ref[:, cols]
            sc = lax.dot_general(q, ck_ref[:, cols], dims, preferred_element_type=jnp.float32) * HD ** (-0.5)
            sn = lax.dot_general(q, nk_ref[:, cols], dims, preferred_element_type=jnp.float32) * HD ** (-0.5)
            sc = jnp.where(live_c, sc, -1e30)
            sn = jnp.where(live_n, sn, -1e30)
            top = jnp.maximum(jnp.max(sc, axis=1, keepdims=True), jnp.max(sn, axis=1, keepdims=True))
            ec = jnp.exp(sc - top)
            en = jnp.exp(sn - top)
            total = jnp.sum(ec, axis=1, keepdims=True) + jnp.sum(en, axis=1, keepdims=True)
            wc = (ec / total).astype(jnp.bfloat16)
            wn = (en / total).astype(jnp.bfloat16)
            att = jnp.dot(wc, cv_ref[:, cols], preferred_element_type=jnp.float32)
            att = att + jnp.dot(wn, nv_ref[:, cols], preferred_element_type=jnp.float32)
            heads.append(att.astype(jnp.bfloat16))
        attended = jnp.concatenate(heads, axis=1)
        partial = jnp.dot(attended, ow_ref[...], preferred_element_type=jnp.float32)
        half = columns // 2
        for k in range(tp_count):
            out_ref[k, 0:tokens, :] = partial[:, k * columns:k * columns + half]
            out_ref[k, tokens:2 * tokens, :] = partial[:, k * columns + half:(k + 1) * columns]

    vmem = pl.BlockSpec(memory_space=pltpu.VMEM)
    return pl.pallas_call(
        kernel,
        out_shape=jax.ShapeDtypeStruct((tp_count, 2 * tokens, columns // 2), jnp.float32),
        in_specs=[pl.BlockSpec(memory_space=pltpu.SMEM)] + [vmem] * 6,
        out_specs=vmem,
    )(cache_lengths, queries, new_keys, new_values, flat_k, flat_v, out_weight)


def expert_apply(slot_rows, gate_weight, up_weight, down_weight):
    slots, width = slot_rows.shape
    hidden = gate_weight.shape[-1]

    def kernel(x_ref, wg_ref, wu_ref, wd_ref, out_ref):
        rows = x_ref[...]
        gated = jnp.dot(rows, wg_ref[...], preferred_element_type=jnp.float32)
        upward = jnp.dot(rows, wu_ref[...], preferred_element_type=jnp.float32)
        activation = (gated / (1.0 + jnp.exp(-gated)) * upward).astype(jnp.bfloat16)
        out_ref[...] = jnp.dot(activation, wd_ref[...], preferred_element_type=jnp.float32).astype(jnp.bfloat16)

    vmem = pl.BlockSpec(memory_space=pltpu.VMEM)
    return pl.pallas_call(
        kernel,
        out_shape=jax.ShapeDtypeStruct((slots, width), jnp.bfloat16),
        in_specs=[vmem] * 4,
        out_specs=vmem,
    )(
        slot_rows,
        gate_weight.reshape(width, hidden),
        up_weight.reshape(width, hidden),
        down_weight.reshape(hidden, width),
    )


def stack_halves(value):
    half = value.shape[1] // 2
    return jnp.concatenate([value[:, :half], value[:, half:]], axis=0)


def unstack_halves(value):
    rows = value.shape[0] // 2
    return jnp.concatenate([value[:rows], value[rows:]], axis=1)


def scatter_sum(value, tp_count):
    rows, width = value.shape
    pieces = value.reshape(rows, tp_count, 2, width // tp_count // 2).transpose(1, 2, 0, 3)
    pieces = pieces.reshape(tp_count, 2 * rows, width // tp_count // 2)
    pieces = lax.all_to_all(pieces, "tp", split_axis=0, concat_axis=0, tiled=True)
    return unstack_halves(jnp.sum(pieces.astype(jnp.float32), axis=0))


def gather_cols(value, tp_count):
    rows, columns = value.shape
    stacked = stack_halves(value)
    pieces = jnp.broadcast_to(stacked[None], (tp_count,) + stacked.shape)
    pieces = lax.all_to_all(pieces, "tp", split_axis=0, concat_axis=0, tiled=True)
    pieces = pieces.reshape(tp_count, 2, rows, columns // 2).transpose(2, 0, 1, 3)
    return pieces.reshape(rows, tp_count * columns)


def local(
    queries,
    new_keys,
    new_values,
    cache_keys,
    cache_values,
    cache_lengths,
    hidden_in,
    out_weight,
    norm_gain,
    routes,
    route_gates,
    gate_weight,
    up_weight,
    down_weight,
):
    model_width = out_weight.shape[1]
    tp_count = lax.axis_size("tp")
    pieces = attend_project(
        queries, new_keys, new_values, cache_keys, cache_values, cache_lengths, out_weight, tp_count
    )
    columns = model_width // tp_count
    offset = lax.axis_index("tp") * columns
    holders = lax.axis_size("req")
    dispatch, combine = slot_tables(routes, route_gates)
    hidden_cols = lax.dynamic_slice_in_dim(hidden_in, offset, columns, 1).astype(jnp.float32)
    pieces = lax.all_to_all(pieces, "tp", split_axis=0, concat_axis=0, tiled=True)
    summed_cols = unstack_halves(jnp.sum(pieces, axis=0)) + hidden_cols
    summed = gather_cols(summed_cols, tp_count)
    mean_square = jnp.mean(summed * summed, axis=-1, keepdims=True)
    normed = (summed * lax.rsqrt(mean_square + 1e-06) * norm_gain[None, :]).astype(jnp.bfloat16)
    outbound = jnp.dot(dispatch, normed, preferred_element_type=jnp.float32).astype(jnp.bfloat16)
    packed = (holders, CAP * model_width // 128, 128)
    outbound = outbound.reshape(packed)
    arrived = lax.all_to_all(outbound, "req", split_axis=0, concat_axis=0, tiled=True)
    produced = expert_apply(
        arrived.reshape(holders * CAP, model_width), gate_weight, up_weight, down_weight
    )
    returned = lax.all_to_all(
        produced.reshape(packed), "req", split_axis=0, concat_axis=0, tiled=True
    ).astype(jnp.float32)
    expert_sum = jnp.dot(
        combine,
        returned.reshape(-1, model_width),
        precision=lax.Precision.HIGHEST,
        preferred_element_type=jnp.float32,
    )
    expert_cols = scatter_sum(expert_sum.astype(jnp.bfloat16), tp_count)
    return (summed_cols + expert_cols).astype(jnp.bfloat16)


def solution(mesh):
    in_specs = (
        P("req", "tp"),
        P("req", "tp"),
        P("req", "tp"),
        P("req", None, "tp"),
        P("req", None, "tp"),
        P("req"),
        P("req", None),
        P("tp", None),
        P(),
        P("req", None),
        P("req", None),
        P("req", None, "tp"),
        P("req", None, "tp"),
        P("req", "tp", None),
    )
    out_specs = P("req", "tp")
    return jax.shard_map(local, mesh=mesh, in_specs=in_specs, out_specs=out_specs, check_vma=False)
```

```python
import jax
import jax.numpy as jnp
from jax import lax
from jax.experimental import pallas as pl
from jax.experimental.pallas import tpu as pltpu
from jax.sharding import PartitionSpec as P

HD = 128
EXPERTS = 64
POS = 5
CACHE = 384
CAP = 3


def slot_tables(local_routes, local_gates):
    flat_routes = local_routes.reshape(-1)
    expert_ids = jnp.arange(EXPERTS, dtype=jnp.int32)
    onehot = (flat_routes[:, None] == expert_ids[None, :]).astype(jnp.int32)
    before = jnp.cumsum(onehot, axis=0) - onehot
    ranks = jnp.sum(before * onehot, axis=1)
    slot_ids = (flat_routes * CAP + ranks).reshape(local_routes.shape)
    slot_range = jnp.arange(EXPERTS * CAP, dtype=jnp.int32)
    matches = slot_ids[None, :, :] == slot_range[:, None, None]
    dispatch = jnp.any(matches, axis=-1).astype(jnp.bfloat16)
    combine = jnp.sum(jnp.where(matches, local_gates[None, :, :], 0.0), axis=-1).T
    return (dispatch, combine)


def attend_project(queries, new_keys, new_values, cache_keys, cache_values, cache_lengths, out_weight, tp_count):
    req_count, cache_len, width = cache_keys.shape
    tokens = queries.shape[0]
    model_width = out_weight.shape[1]
    columns = model_width // tp_count
    head_count = width // HD
    flat_k = cache_keys.reshape(req_count * cache_len, width)
    flat_v = cache_values.reshape(req_count * cache_len, width)

    def kernel(len_ref, q_ref, nk_ref, nv_ref, ck_ref, cv_ref, ow_ref, out_ref):
        row = lax.broadcasted_iota(jnp.int32, (tokens, 1), 0)
        lo = jnp.zeros((tokens, 1), jnp.int32)
        hi = jnp.zeros((tokens, 1), jnp.int32)
        first = jnp.zeros((tokens, 1), jnp.int32)
        for r in range(req_count):
            mine = (row >= r * POS) & (row < (r + 1) * POS)
            lo = jnp.where(mine, r * cache_len, lo)
            hi = jnp.where(mine, r * cache_len + len_ref[r], hi)
            first = jnp.where(mine, r * POS, first)
        key_at = lax.broadcasted_iota(jnp.int32, (tokens, req_count * cache_len), 1)
        live_c = (key_at >= lo) & (key_at < hi)
        fresh_at = lax.broadcasted_iota(jnp.int32, (tokens, tokens), 1)
        live_n = (fresh_at >= first) & (fresh_at <= row)
        dims = (((1,), (1,)), ((), ()))
        heads = []
        for h in range(head_count):
            cols = slice(h * HD, (h + 1) * HD)
            q = q_ref[:, cols]
            sc = lax.dot_general(q, ck_ref[:, cols], dims, preferred_element_type=jnp.float32) * HD ** (-0.5)
            sn = lax.dot_general(q, nk_ref[:, cols], dims, preferred_element_type=jnp.float32) * HD ** (-0.5)
            sc = jnp.where(live_c, sc, -1e30)
            sn = jnp.where(live_n, sn, -1e30)
            top = jnp.maximum(jnp.max(sc, axis=1, keepdims=True), jnp.max(sn, axis=1, keepdims=True))
            ec = jnp.exp(sc - top)
            en = jnp.exp(sn - top)
            total = jnp.sum(ec, axis=1, keepdims=True) + jnp.sum(en, axis=1, keepdims=True)
            wc = (ec / total).astype(jnp.bfloat16)
            wn = (en / total).astype(jnp.bfloat16)
            att = jnp.dot(wc, cv_ref[:, cols], preferred_element_type=jnp.float32)
            att = att + jnp.dot(wn, nv_ref[:, cols], preferred_element_type=jnp.float32)
            heads.append(att.astype(jnp.bfloat16))
        attended = jnp.concatenate(heads, axis=1)
        partial = jnp.dot(attended, ow_ref[...], preferred_element_type=jnp.float32)
        half = columns // 2
        for k in range(tp_count):
            out_ref[k, 0:tokens, :] = partial[:, k * columns:k * columns + half]
            out_ref[k, tokens:2 * tokens, :] = partial[:, k * columns + half:(k + 1) * columns]

    vmem = pl.BlockSpec(memory_space=pltpu.VMEM)
    return pl.pallas_call(
        kernel,
        out_shape=jax.ShapeDtypeStruct((tp_count, 2 * tokens, columns // 2), jnp.float32),
        in_specs=[pl.BlockSpec(memory_space=pltpu.SMEM)] + [vmem] * 6,
        out_specs=vmem,
    )(cache_lengths, queries, new_keys, new_values, flat_k, flat_v, out_weight)


def expert_apply(slot_rows, gate_weight, up_weight, down_weight):
    gated = jnp.einsum("secd,edf->secf", slot_rows, gate_weight, preferred_element_type=jnp.float32)
    upward = jnp.einsum("secd,edf->secf", slot_rows, up_weight, preferred_element_type=jnp.float32)
    activation = (jax.nn.silu(gated) * upward).astype(jnp.bfloat16)
    slots = activation.shape[0] * activation.shape[1] * activation.shape[2]
    hidden = activation.shape[3]
    width = down_weight.shape[2]
    return jnp.einsum(
        "sf,fkl->skl",
        activation.reshape(slots, hidden),
        down_weight.reshape(hidden, width // 128, 128),
        preferred_element_type=jnp.float32,
    )


def stack_halves(value):
    half = value.shape[1] // 2
    return jnp.concatenate([value[:, :half], value[:, half:]], axis=0)


def unstack_halves(value):
    rows = value.shape[0] // 2
    return jnp.concatenate([value[:rows], value[rows:]], axis=1)


def scatter_sum(value, tp_count):
    rows, width = value.shape
    pieces = value.reshape(rows, tp_count, 2, width // tp_count // 2).transpose(1, 2, 0, 3)
    pieces = pieces.reshape(tp_count, 2 * rows, width // tp_count // 2)
    pieces = lax.all_to_all(pieces, "tp", split_axis=0, concat_axis=0, tiled=True)
    return unstack_halves(jnp.sum(pieces.astype(jnp.float32), axis=0))


def gather_cols(value, tp_count):
    rows, columns = value.shape
    stacked = stack_halves(value)
    pieces = jnp.broadcast_to(stacked[None], (tp_count,) + stacked.shape)
    pieces = lax.all_to_all(pieces, "tp", split_axis=0, concat_axis=0, tiled=True)
    pieces = pieces.reshape(tp_count, 2, rows, columns // 2).transpose(2, 0, 1, 3)
    return pieces.reshape(rows, tp_count * columns)


def local(
    queries,
    new_keys,
    new_values,
    cache_keys,
    cache_values,
    cache_lengths,
    hidden_in,
    out_weight,
    norm_gain,
    routes,
    route_gates,
    gate_weight,
    up_weight,
    down_weight,
):
    model_width = out_weight.shape[1]
    tp_count = lax.axis_size("tp")
    pieces = attend_project(
        queries, new_keys, new_values, cache_keys, cache_values, cache_lengths, out_weight, tp_count
    )
    columns = model_width // tp_count
    offset = lax.axis_index("tp") * columns
    holders = lax.axis_size("req")
    dispatch, combine = slot_tables(routes, route_gates)
    hidden_cols = lax.dynamic_slice_in_dim(hidden_in, offset, columns, 1).astype(jnp.float32)
    pieces = lax.all_to_all(pieces, "tp", split_axis=0, concat_axis=0, tiled=True)
    summed_cols = unstack_halves(jnp.sum(pieces, axis=0)) + hidden_cols
    summed = gather_cols(summed_cols, tp_count)
    mean_square = jnp.mean(summed * summed, axis=-1, keepdims=True)
    normed = (summed * lax.rsqrt(mean_square + 1e-06) * norm_gain[None, :]).astype(jnp.bfloat16)
    outbound = jnp.dot(dispatch, normed, preferred_element_type=jnp.float32).astype(jnp.bfloat16)
    packed = (holders, CAP * model_width // 128, 128)
    outbound = outbound.reshape(packed)
    arrived = lax.all_to_all(outbound, "req", split_axis=0, concat_axis=0, tiled=True)
    produced = expert_apply(
        arrived.reshape(holders, 1, CAP, model_width),
        gate_weight,
        up_weight,
        down_weight,
    )
    returned = lax.all_to_all(
        produced.astype(jnp.bfloat16).reshape(packed), "req", split_axis=0, concat_axis=0, tiled=True
    ).astype(jnp.float32)
    expert_sum = jnp.dot(
        combine,
        returned.reshape(-1, model_width),
        precision=lax.Precision.HIGHEST,
        preferred_element_type=jnp.float32,
    )
    expert_cols = scatter_sum(expert_sum.astype(jnp.bfloat16), tp_count)
    return (summed_cols + expert_cols).astype(jnp.bfloat16)


def solution(mesh):
    in_specs = (
        P("req", "tp"),
        P("req", "tp"),
        P("req", "tp"),
        P("req", None, "tp"),
        P("req", None, "tp"),
        P("req"),
        P("req", None),
        P("tp", None),
        P(),
        P("req", None),
        P("req", None),
        P("req", None, "tp"),
        P("req", None, "tp"),
        P("req", "tp", None),
    )
    out_specs = P("req", "tp")
    return jax.shard_map(local, mesh=mesh, in_specs=in_specs, out_specs=out_specs, check_vma=False)
```

```python
import jax
import jax.numpy as jnp
from jax import lax
from jax.experimental import pallas as pl
from jax.experimental.pallas import tpu as pltpu
from jax.sharding import PartitionSpec as P

HD = 128
EXPERTS = 64
POS = 5
CACHE = 384
CAP = 3


def slot_tables(local_routes, local_gates):
    flat_routes = local_routes.reshape(-1)
    expert_ids = jnp.arange(EXPERTS, dtype=jnp.int32)
    onehot = (flat_routes[:, None] == expert_ids[None, :]).astype(jnp.int32)
    before = jnp.cumsum(onehot, axis=0) - onehot
    ranks = jnp.sum(before * onehot, axis=1)
    slot_ids = (flat_routes * CAP + ranks).reshape(local_routes.shape)
    slot_range = jnp.arange(EXPERTS * CAP, dtype=jnp.int32)
    matches = slot_ids[None, :, :] == slot_range[:, None, None]
    dispatch = jnp.any(matches, axis=-1).astype(jnp.bfloat16)
    combine = jnp.sum(jnp.where(matches, local_gates[None, :, :], 0.0), axis=-1).T
    return (dispatch, combine)


def attend_project(queries, new_keys, new_values, cache_keys, cache_values, cache_lengths, out_weight, tp_count):
    req_count, cache_len, width = cache_keys.shape
    tokens = queries.shape[0]
    model_width = out_weight.shape[1]
    columns = model_width // tp_count
    head_count = width // HD
    flat_k = cache_keys.reshape(req_count * cache_len, width)
    flat_v = cache_values.reshape(req_count * cache_len, width)

    def kernel(len_ref, q_ref, nk_ref, nv_ref, ck_ref, cv_ref, ow_ref, out_ref):
        head = pl.program_id(0)
        row = lax.broadcasted_iota(jnp.int32, (tokens, 1), 0)
        lo = jnp.zeros((tokens, 1), jnp.int32)
        hi = jnp.zeros((tokens, 1), jnp.int32)
        first = jnp.zeros((tokens, 1), jnp.int32)
        for r in range(req_count):
            mine = (row >= r * POS) & (row < (r + 1) * POS)
            lo = jnp.where(mine, r * cache_len, lo)
            hi = jnp.where(mine, r * cache_len + len_ref[r], hi)
            first = jnp.where(mine, r * POS, first)
        key_at = lax.broadcasted_iota(jnp.int32, (tokens, req_count * cache_len), 1)
        live_c = (key_at >= lo) & (key_at < hi)
        fresh_at = lax.broadcasted_iota(jnp.int32, (tokens, tokens), 1)
        live_n = (fresh_at >= first) & (fresh_at <= row)
        dims = (((1,), (1,)), ((), ()))
        q = q_ref[...]
        sc = lax.dot_general(q, ck_ref[...], dims, preferred_element_type=jnp.float32) * HD ** (-0.5)
        sn = lax.dot_general(q, nk_ref[...], dims, preferred_element_type=jnp.float32) * HD ** (-0.5)
        sc = jnp.where(live_c, sc, -1e30)
        sn = jnp.where(live_n, sn, -1e30)
        top = jnp.maximum(jnp.max(sc, axis=1, keepdims=True), jnp.max(sn, axis=1, keepdims=True))
        ec = jnp.exp(sc - top)
        en = jnp.exp(sn - top)
        total = jnp.sum(ec, axis=1, keepdims=True) + jnp.sum(en, axis=1, keepdims=True)
        wc = (ec / total).astype(jnp.bfloat16)
        wn = (en / total).astype(jnp.bfloat16)
        att = jnp.dot(wc, cv_ref[...], preferred_element_type=jnp.float32)
        att = att + jnp.dot(wn, nv_ref[...], preferred_element_type=jnp.float32)
        partial = jnp.dot(att.astype(jnp.bfloat16), ow_ref[...], preferred_element_type=jnp.float32)
        half = columns // 2

        @pl.when(head == 0)
        def _():
            for k in range(tp_count):
                out_ref[k, 0:tokens, :] = partial[:, k * columns:k * columns + half]
                out_ref[k, tokens:2 * tokens, :] = partial[:, k * columns + half:(k + 1) * columns]

        @pl.when(head > 0)
        def _():
            for k in range(tp_count):
                out_ref[k, 0:tokens, :] += partial[:, k * columns:k * columns + half]
                out_ref[k, tokens:2 * tokens, :] += partial[:, k * columns + half:(k + 1) * columns]

    token_block = pl.BlockSpec((tokens, HD), lambda h: (0, h))
    cache_block = pl.BlockSpec((req_count * cache_len, HD), lambda h: (0, h))
    return pl.pallas_call(
        kernel,
        grid=(head_count,),
        out_shape=jax.ShapeDtypeStruct((tp_count, 2 * tokens, columns // 2), jnp.float32),
        in_specs=[
            pl.BlockSpec(memory_space=pltpu.SMEM),
            token_block,
            token_block,
            token_block,
            cache_block,
            cache_block,
            pl.BlockSpec((HD, model_width), lambda h: (h, 0)),
        ],
        out_specs=pl.BlockSpec((tp_count, 2 * tokens, columns // 2), lambda h: (0, 0, 0)),
    )(cache_lengths, queries, new_keys, new_values, flat_k, flat_v, out_weight)


def expert_apply(slot_rows, gate_weight, up_weight, down_weight):
    gated = jnp.einsum("secd,edf->secf", slot_rows, gate_weight, preferred_element_type=jnp.float32)
    upward = jnp.einsum("secd,edf->secf", slot_rows, up_weight, preferred_element_type=jnp.float32)
    activation = (jax.nn.silu(gated) * upward).astype(jnp.bfloat16)
    slots = activation.shape[0] * activation.shape[1] * activation.shape[2]
    hidden = activation.shape[3]
    width = down_weight.shape[2]
    return jnp.einsum(
        "sf,fkl->skl",
        activation.reshape(slots, hidden),
        down_weight.reshape(hidden, width // 128, 128),
        preferred_element_type=jnp.float32,
    )


def stack_halves(value):
    half = value.shape[1] // 2
    return jnp.concatenate([value[:, :half], value[:, half:]], axis=0)


def unstack_halves(value):
    rows = value.shape[0] // 2
    return jnp.concatenate([value[:rows], value[rows:]], axis=1)


def scatter_sum(value, tp_count):
    rows, width = value.shape
    pieces = value.reshape(rows, tp_count, 2, width // tp_count // 2).transpose(1, 2, 0, 3)
    pieces = pieces.reshape(tp_count, 2 * rows, width // tp_count // 2)
    pieces = lax.all_to_all(pieces, "tp", split_axis=0, concat_axis=0, tiled=True)
    return unstack_halves(jnp.sum(pieces.astype(jnp.float32), axis=0))


def gather_cols(value, tp_count):
    rows, columns = value.shape
    stacked = stack_halves(value)
    pieces = jnp.broadcast_to(stacked[None], (tp_count,) + stacked.shape)
    pieces = lax.all_to_all(pieces, "tp", split_axis=0, concat_axis=0, tiled=True)
    pieces = pieces.reshape(tp_count, 2, rows, columns // 2).transpose(2, 0, 1, 3)
    return pieces.reshape(rows, tp_count * columns)


def local(
    queries,
    new_keys,
    new_values,
    cache_keys,
    cache_values,
    cache_lengths,
    hidden_in,
    out_weight,
    norm_gain,
    routes,
    route_gates,
    gate_weight,
    up_weight,
    down_weight,
):
    model_width = out_weight.shape[1]
    tp_count = lax.axis_size("tp")
    pieces = attend_project(
        queries, new_keys, new_values, cache_keys, cache_values, cache_lengths, out_weight, tp_count
    )
    columns = model_width // tp_count
    offset = lax.axis_index("tp") * columns
    holders = lax.axis_size("req")
    dispatch, combine = slot_tables(routes, route_gates)
    hidden_cols = lax.dynamic_slice_in_dim(hidden_in, offset, columns, 1).astype(jnp.float32)
    pieces = lax.all_to_all(pieces, "tp", split_axis=0, concat_axis=0, tiled=True)
    summed_cols = unstack_halves(jnp.sum(pieces, axis=0)) + hidden_cols
    summed = gather_cols(summed_cols, tp_count)
    mean_square = jnp.mean(summed * summed, axis=-1, keepdims=True)
    normed = (summed * lax.rsqrt(mean_square + 1e-06) * norm_gain[None, :]).astype(jnp.bfloat16)
    outbound = jnp.dot(dispatch, normed, preferred_element_type=jnp.float32).astype(jnp.bfloat16)
    packed = (holders, CAP * model_width // 128, 128)
    outbound = outbound.reshape(packed)
    arrived = lax.all_to_all(outbound, "req", split_axis=0, concat_axis=0, tiled=True)
    produced = expert_apply(
        arrived.reshape(holders, 1, CAP, model_width),
        gate_weight,
        up_weight,
        down_weight,
    )
    returned = lax.all_to_all(
        produced.astype(jnp.bfloat16).reshape(packed), "req", split_axis=0, concat_axis=0, tiled=True
    ).astype(jnp.float32)
    expert_sum = jnp.dot(
        combine,
        returned.reshape(-1, model_width),
        precision=lax.Precision.HIGHEST,
        preferred_element_type=jnp.float32,
    )
    expert_cols = scatter_sum(expert_sum.astype(jnp.bfloat16), tp_count)
    return (summed_cols + expert_cols).astype(jnp.bfloat16)


def solution(mesh):
    in_specs = (
        P("req", "tp"),
        P("req", "tp"),
        P("req", "tp"),
        P("req", None, "tp"),
        P("req", None, "tp"),
        P("req"),
        P("req", None),
        P("tp", None),
        P(),
        P("req", None),
        P("req", None),
        P("req", None, "tp"),
        P("req", None, "tp"),
        P("req", "tp", None),
    )
    out_specs = P("req", "tp")
    return jax.shard_map(local, mesh=mesh, in_specs=in_specs, out_specs=out_specs, check_vma=False)
```

```python
import jax
import jax.numpy as jnp
from jax import lax
from jax.experimental import pallas as pl
from jax.experimental.pallas import tpu as pltpu
from jax.sharding import PartitionSpec as P

HD = 128
EXPERTS = 64
POS = 5
CACHE = 384
CAP = 3


def slot_tables(local_routes, local_gates):
    flat_routes = local_routes.reshape(-1)
    expert_ids = jnp.arange(EXPERTS, dtype=jnp.int32)
    onehot = (flat_routes[:, None] == expert_ids[None, :]).astype(jnp.int32)
    before = jnp.cumsum(onehot, axis=0) - onehot
    ranks = jnp.sum(before * onehot, axis=1)
    slot_ids = (flat_routes * CAP + ranks).reshape(local_routes.shape)
    slot_range = jnp.arange(EXPERTS * CAP, dtype=jnp.int32)
    matches = slot_ids[None, :, :] == slot_range[:, None, None]
    dispatch = jnp.any(matches, axis=-1).astype(jnp.bfloat16)
    combine = jnp.sum(jnp.where(matches, local_gates[None, :, :], 0.0), axis=-1).T
    return (dispatch, combine)


def attend_project(queries, new_keys, new_values, cache_keys, cache_values, cache_lengths, out_weight, tp_count):
    req_count, cache_len, width = cache_keys.shape
    tokens = queries.shape[0]
    model_width = out_weight.shape[1]
    columns = model_width // tp_count
    head_count = width // HD
    flat_k = cache_keys.reshape(req_count * cache_len, width)
    flat_v = cache_values.reshape(req_count * cache_len, width)

    def kernel(len_ref, q_ref, nk_ref, nv_ref, ck_ref, cv_ref, ow_ref, out_ref):
        row = lax.broadcasted_iota(jnp.int32, (tokens, 1), 0)
        lo = jnp.zeros((tokens, 1), jnp.int32)
        hi = jnp.zeros((tokens, 1), jnp.int32)
        first = jnp.zeros((tokens, 1), jnp.int32)
        for r in range(req_count):
            mine = (row >= r * POS) & (row < (r + 1) * POS)
            lo = jnp.where(mine, r * cache_len, lo)
            hi = jnp.where(mine, r * cache_len + len_ref[r], hi)
            first = jnp.where(mine, r * POS, first)
        key_at = lax.broadcasted_iota(jnp.int32, (tokens, req_count * cache_len), 1)
        live_c = (key_at >= lo) & (key_at < hi)
        fresh_at = lax.broadcasted_iota(jnp.int32, (tokens, tokens), 1)
        live_n = (fresh_at >= first) & (fresh_at <= row)
        dims = (((1,), (1,)), ((), ()))
        heads = []
        for h in range(head_count):
            cols = slice(h * HD, (h + 1) * HD)
            q = q_ref[:, cols]
            sc = lax.dot_general(q, ck_ref[:, cols], dims, preferred_element_type=jnp.float32) * HD ** (-0.5)
            sn = lax.dot_general(q, nk_ref[:, cols], dims, preferred_element_type=jnp.float32) * HD ** (-0.5)
            sc = jnp.where(live_c, sc, -1e30)
            sn = jnp.where(live_n, sn, -1e30)
            top = jnp.maximum(jnp.max(sc, axis=1, keepdims=True), jnp.max(sn, axis=1, keepdims=True))
            ec = jnp.exp(sc - top)
            en = jnp.exp(sn - top)
            total = jnp.sum(ec, axis=1, keepdims=True) + jnp.sum(en, axis=1, keepdims=True)
            wc = (ec / total).astype(jnp.bfloat16)
            wn = (en / total).astype(jnp.bfloat16)
            att = jnp.dot(wc, cv_ref[:, cols], preferred_element_type=jnp.float32)
            att = att + jnp.dot(wn, nv_ref[:, cols], preferred_element_type=jnp.float32)
            heads.append(att.astype(jnp.bfloat16))
        attended = jnp.concatenate(heads, axis=1)
        partial = jnp.dot(attended, ow_ref[...], preferred_element_type=jnp.float32)
        half = columns // 2
        for k in range(tp_count):
            out_ref[k, 0:tokens, :] = partial[:, k * columns:k * columns + half]
            out_ref[k, tokens:2 * tokens, :] = partial[:, k * columns + half:(k + 1) * columns]

    vmem = pl.BlockSpec(memory_space=pltpu.VMEM)
    return pl.pallas_call(
        kernel,
        out_shape=jax.ShapeDtypeStruct((tp_count, 2 * tokens, columns // 2), jnp.float32),
        in_specs=[pl.BlockSpec(memory_space=pltpu.SMEM)] + [vmem] * 6,
        out_specs=vmem,
    )(cache_lengths, queries, new_keys, new_values, flat_k, flat_v, out_weight)


def expert_apply(slot_rows, gate_weight, up_weight, down_weight):
    width, hidden = gate_weight.shape[1], gate_weight.shape[2]
    gated = jnp.dot(slot_rows, gate_weight.reshape(width, hidden), preferred_element_type=jnp.float32)
    upward = jnp.dot(slot_rows, up_weight.reshape(width, hidden), preferred_element_type=jnp.float32)
    activation = (jax.nn.silu(gated) * upward).astype(jnp.bfloat16)
    return jnp.einsum(
        "sf,fkl->skl",
        activation,
        down_weight.reshape(hidden, width // 128, 128),
        preferred_element_type=jnp.float32,
    )


def stack_halves(value):
    half = value.shape[1] // 2
    return jnp.concatenate([value[:, :half], value[:, half:]], axis=0)


def unstack_halves(value):
    rows = value.shape[0] // 2
    return jnp.concatenate([value[:rows], value[rows:]], axis=1)


def scatter_sum(value, tp_count):
    rows, width = value.shape
    pieces = value.reshape(rows, tp_count, 2, width // tp_count // 2).transpose(1, 2, 0, 3)
    pieces = pieces.reshape(tp_count, 2 * rows, width // tp_count // 2)
    pieces = lax.all_to_all(pieces, "tp", split_axis=0, concat_axis=0, tiled=True)
    return unstack_halves(jnp.sum(pieces.astype(jnp.float32), axis=0))


def gather_stacked(stacked, tp_count):
    rows, half = stacked.shape[0] // 2, stacked.shape[1]
    pieces = jnp.broadcast_to(stacked[None], (tp_count,) + stacked.shape)
    pieces = lax.all_to_all(pieces, "tp", split_axis=0, concat_axis=0, tiled=True)
    pieces = pieces.reshape(tp_count, 2, rows, half).transpose(2, 0, 1, 3)
    return pieces.reshape(rows, tp_count * 2 * half)


def local(
    queries,
    new_keys,
    new_values,
    cache_keys,
    cache_values,
    cache_lengths,
    hidden_in,
    out_weight,
    norm_gain,
    routes,
    route_gates,
    gate_weight,
    up_weight,
    down_weight,
):
    model_width = out_weight.shape[1]
    tp_count = lax.axis_size("tp")
    pieces = attend_project(
        queries, new_keys, new_values, cache_keys, cache_values, cache_lengths, out_weight, tp_count
    )
    columns = model_width // tp_count
    offset = lax.axis_index("tp") * columns
    holders = lax.axis_size("req")
    dispatch, combine = slot_tables(routes, route_gates)
    hidden_cols = lax.dynamic_slice_in_dim(hidden_in, offset, columns, 1).astype(jnp.float32)
    pieces = lax.all_to_all(pieces, "tp", split_axis=0, concat_axis=0, tiled=True)
    summed_stacked = jnp.sum(pieces, axis=0) + stack_halves(hidden_cols)
    summed_cols = unstack_halves(summed_stacked)
    summed = gather_stacked(summed_stacked, tp_count)
    mean_square = jnp.mean(summed * summed, axis=-1, keepdims=True)
    normed = (summed * lax.rsqrt(mean_square + 1e-06) * norm_gain[None, :]).astype(jnp.bfloat16)
    outbound = jnp.dot(dispatch, normed, preferred_element_type=jnp.float32).astype(jnp.bfloat16)
    packed = (holders, CAP * model_width // 128, 128)
    outbound = outbound.reshape(packed)
    arrived = lax.all_to_all(outbound, "req", split_axis=0, concat_axis=0, tiled=True)
    produced = expert_apply(
        arrived.reshape(holders * CAP, model_width),
        gate_weight,
        up_weight,
        down_weight,
    )
    returned = lax.all_to_all(
        produced.astype(jnp.bfloat16).reshape(packed), "req", split_axis=0, concat_axis=0, tiled=True
    ).astype(jnp.float32)
    expert_sum = jnp.dot(
        combine,
        returned.reshape(-1, model_width),
        precision=lax.Precision.HIGHEST,
        preferred_element_type=jnp.float32,
    )
    expert_cols = scatter_sum(expert_sum.astype(jnp.bfloat16), tp_count)
    return (summed_cols + expert_cols).astype(jnp.bfloat16)


def solution(mesh):
    in_specs = (
        P("req", "tp"),
        P("req", "tp"),
        P("req", "tp"),
        P("req", None, "tp"),
        P("req", None, "tp"),
        P("req"),
        P("req", None),
        P("tp", None),
        P(),
        P("req", None),
        P("req", None),
        P("req", None, "tp"),
        P("req", None, "tp"),
        P("req", "tp", None),
    )
    out_specs = P("req", "tp")
    return jax.shard_map(local, mesh=mesh, in_specs=in_specs, out_specs=out_specs, check_vma=False)
```

```python
import jax
import jax.numpy as jnp
from jax import lax
from jax.experimental import pallas as pl
from jax.experimental.pallas import tpu as pltpu
from jax.sharding import PartitionSpec as P

HD = 128
EXPERTS = 64
POS = 5
CACHE = 384
CAP = 3


def slot_tables(local_routes, local_gates):
    flat_routes = local_routes.reshape(-1)
    expert_ids = jnp.arange(EXPERTS, dtype=jnp.int32)
    onehot = (flat_routes[:, None] == expert_ids[None, :]).astype(jnp.int32)
    before = jnp.cumsum(onehot, axis=0) - onehot
    ranks = jnp.sum(before * onehot, axis=1)
    slot_ids = (flat_routes * CAP + ranks).reshape(local_routes.shape)
    slot_range = jnp.arange(EXPERTS * CAP, dtype=jnp.int32)
    matches = slot_ids[None, :, :] == slot_range[:, None, None]
    dispatch = jnp.any(matches, axis=-1).astype(jnp.bfloat16)
    combine = jnp.sum(jnp.where(matches, local_gates[None, :, :], 0.0), axis=-1).T
    return (dispatch, combine)


def attend_project(queries, new_keys, new_values, cache_keys, cache_values, cache_lengths, out_weight, tp_count):
    req_count, cache_len, width = cache_keys.shape
    tokens = queries.shape[0]
    model_width = out_weight.shape[1]
    columns = model_width // tp_count
    head_count = width // HD
    flat_k = cache_keys.reshape(req_count * cache_len, width)
    flat_v = cache_values.reshape(req_count * cache_len, width)

    def kernel(len_ref, q_ref, nk_ref, nv_ref, ck_ref, cv_ref, ow_ref, out_ref):
        row = lax.broadcasted_iota(jnp.int32, (tokens, 1), 0)
        lo = jnp.zeros((tokens, 1), jnp.int32)
        hi = jnp.zeros((tokens, 1), jnp.int32)
        first = jnp.zeros((tokens, 1), jnp.int32)
        for r in range(req_count):
            mine = (row >= r * POS) & (row < (r + 1) * POS)
            lo = jnp.where(mine, r * cache_len, lo)
            hi = jnp.where(mine, r * cache_len + len_ref[r], hi)
            first = jnp.where(mine, r * POS, first)
        key_at = lax.broadcasted_iota(jnp.int32, (tokens, req_count * cache_len), 1)
        live_c = (key_at >= lo) & (key_at < hi)
        fresh_at = lax.broadcasted_iota(jnp.int32, (tokens, tokens), 1)
        live_n = (fresh_at >= first) & (fresh_at <= row)
        dims = (((1,), (1,)), ((), ()))
        heads = []
        for h in range(head_count):
            cols = slice(h * HD, (h + 1) * HD)
            q = q_ref[:, cols]
            sc = lax.dot_general(q, ck_ref[:, cols], dims, preferred_element_type=jnp.float32) * HD ** (-0.5)
            sn = lax.dot_general(q, nk_ref[:, cols], dims, preferred_element_type=jnp.float32) * HD ** (-0.5)
            sc = jnp.where(live_c, sc, -1e30)
            sn = jnp.where(live_n, sn, -1e30)
            top = jnp.maximum(jnp.max(sc, axis=1, keepdims=True), jnp.max(sn, axis=1, keepdims=True))
            ec = jnp.exp(sc - top)
            en = jnp.exp(sn - top)
            total = jnp.sum(ec, axis=1, keepdims=True) + jnp.sum(en, axis=1, keepdims=True)
            wc = (ec / total).astype(jnp.bfloat16)
            wn = (en / total).astype(jnp.bfloat16)
            att = jnp.dot(wc, cv_ref[:, cols], preferred_element_type=jnp.float32)
            att = att + jnp.dot(wn, nv_ref[:, cols], preferred_element_type=jnp.float32)
            heads.append(att.astype(jnp.bfloat16))
        attended = jnp.concatenate(heads, axis=1)
        partial = jnp.dot(attended, ow_ref[...], preferred_element_type=jnp.float32)
        half = columns // 2
        for k in range(tp_count):
            out_ref[k, 0:tokens, :] = partial[:, k * columns:k * columns + half]
            out_ref[k, tokens:2 * tokens, :] = partial[:, k * columns + half:(k + 1) * columns]

    vmem = pl.BlockSpec(memory_space=pltpu.VMEM)
    return pl.pallas_call(
        kernel,
        out_shape=jax.ShapeDtypeStruct((tp_count, 2 * tokens, columns // 2), jnp.float32),
        in_specs=[pl.BlockSpec(memory_space=pltpu.SMEM)] + [vmem] * 6,
        out_specs=vmem,
    )(cache_lengths, queries, new_keys, new_values, flat_k, flat_v, out_weight)


def expert_apply(slot_rows, gate_weight, up_weight, down_weight):
    gated = jnp.einsum("secd,edf->secf", slot_rows, gate_weight, preferred_element_type=jnp.float32)
    upward = jnp.einsum("secd,edf->secf", slot_rows, up_weight, preferred_element_type=jnp.float32)
    activation = (jax.nn.silu(gated) * upward).astype(jnp.bfloat16)
    slots = activation.shape[0] * activation.shape[1] * activation.shape[2]
    hidden = activation.shape[3]
    width = down_weight.shape[2]
    return jnp.einsum(
        "sf,fkl->skl",
        activation.reshape(slots, hidden),
        down_weight.reshape(hidden, width // 128, 128),
        preferred_element_type=jnp.float32,
    )


def stack_halves(value):
    half = value.shape[1] // 2
    return jnp.concatenate([value[:, :half], value[:, half:]], axis=0)


def unstack_halves(value):
    rows = value.shape[0] // 2
    return jnp.concatenate([value[:rows], value[rows:]], axis=1)


def scatter_sum(value, tp_count):
    rows, width = value.shape
    pieces = value.reshape(rows, tp_count, 2, width // tp_count // 2).transpose(1, 2, 0, 3)
    pieces = pieces.reshape(tp_count, 2 * rows, width // tp_count // 2)
    pieces = lax.all_to_all(pieces, "tp", split_axis=0, concat_axis=0, tiled=True)
    return unstack_halves(jnp.sum(pieces.astype(jnp.float32), axis=0))


def gather_cols(value, tp_count):
    rows, columns = value.shape
    stacked = stack_halves(value)
    pieces = jnp.broadcast_to(stacked[None], (tp_count,) + stacked.shape)
    pieces = lax.all_to_all(pieces, "tp", split_axis=0, concat_axis=0, tiled=True)
    pieces = pieces.reshape(tp_count, 2, rows, columns // 2).transpose(2, 0, 1, 3)
    return pieces.reshape(rows, tp_count * columns)


def local(
    queries,
    new_keys,
    new_values,
    cache_keys,
    cache_values,
    cache_lengths,
    hidden_in,
    out_weight,
    norm_gain,
    routes,
    route_gates,
    gate_weight,
    up_weight,
    down_weight,
):
    model_width = out_weight.shape[1]
    tp_count = lax.axis_size("tp")
    pieces = attend_project(
        queries, new_keys, new_values, cache_keys, cache_values, cache_lengths, out_weight, tp_count
    )
    columns = model_width // tp_count
    offset = lax.axis_index("tp") * columns
    holders = lax.axis_size("req")
    dispatch, combine = slot_tables(routes, route_gates)
    hidden_cols = lax.dynamic_slice_in_dim(hidden_in, offset, columns, 1).astype(jnp.float32)
    pieces = lax.all_to_all(pieces, "tp", split_axis=0, concat_axis=0, tiled=True)
    summed_cols = unstack_halves(jnp.sum(pieces, axis=0)) + hidden_cols
    summed = gather_cols(summed_cols, tp_count)
    mean_square = jnp.mean(summed * summed, axis=-1, keepdims=True)
    normed = (summed * lax.rsqrt(mean_square + 1e-06) * norm_gain[None, :]).astype(jnp.bfloat16)
    token_count = normed.shape[0]
    slot_token = jnp.dot(
        dispatch, jnp.arange(1, token_count + 1, dtype=jnp.bfloat16), preferred_element_type=jnp.float32
    ).astype(jnp.int32)
    row_tiles = jnp.concatenate(
        [jnp.zeros((1, model_width // 128, 128), normed.dtype), normed.reshape(token_count, model_width // 128, 128)]
    )
    outbound = jnp.take(row_tiles, slot_token, axis=0, mode="clip")
    packed = (holders, CAP * model_width // 128, 128)
    outbound = outbound.reshape(packed)
    arrived = lax.all_to_all(outbound, "req", split_axis=0, concat_axis=0, tiled=True)
    produced = expert_apply(
        arrived.reshape(holders, 1, CAP, model_width),
        gate_weight,
        up_weight,
        down_weight,
    )
    returned = lax.all_to_all(
        produced.astype(jnp.bfloat16).reshape(packed), "req", split_axis=0, concat_axis=0, tiled=True
    ).astype(jnp.float32)
    expert_sum = jnp.dot(
        combine,
        returned.reshape(-1, model_width),
        precision=lax.Precision.HIGHEST,
        preferred_element_type=jnp.float32,
    )
    expert_cols = scatter_sum(expert_sum.astype(jnp.bfloat16), tp_count)
    return (summed_cols + expert_cols).astype(jnp.bfloat16)


def solution(mesh):
    in_specs = (
        P("req", "tp"),
        P("req", "tp"),
        P("req", "tp"),
        P("req", None, "tp"),
        P("req", None, "tp"),
        P("req"),
        P("req", None),
        P("tp", None),
        P(),
        P("req", None),
        P("req", None),
        P("req", None, "tp"),
        P("req", None, "tp"),
        P("req", "tp", None),
    )
    out_specs = P("req", "tp")
    return jax.shard_map(local, mesh=mesh, in_specs=in_specs, out_specs=out_specs, check_vma=False)
```

```python
import jax
import jax.numpy as jnp
from jax import lax
from jax.experimental import pallas as pl
from jax.experimental.pallas import tpu as pltpu
from jax.sharding import PartitionSpec as P

HD = 128
EXPERTS = 64
POS = 5
CACHE = 384
CAP = 3


def slot_tables(local_routes, local_gates):
    flat_routes = local_routes.reshape(-1)
    expert_ids = jnp.arange(EXPERTS, dtype=jnp.int32)
    onehot = (flat_routes[:, None] == expert_ids[None, :]).astype(jnp.int32)
    before = jnp.cumsum(onehot, axis=0) - onehot
    ranks = jnp.sum(before * onehot, axis=1)
    slot_ids = (flat_routes * CAP + ranks).reshape(local_routes.shape)
    slot_range = jnp.arange(EXPERTS * CAP, dtype=jnp.int32)
    matches = slot_ids[None, :, :] == slot_range[:, None, None]
    dispatch = jnp.any(matches, axis=-1).astype(jnp.bfloat16)
    combine = jnp.sum(jnp.where(matches, local_gates[None, :, :], 0.0), axis=-1).T
    return (dispatch, combine, slot_ids)


def attend_project(queries, new_keys, new_values, cache_keys, cache_values, cache_lengths, out_weight, tp_count):
    req_count, cache_len, width = cache_keys.shape
    tokens = queries.shape[0]
    model_width = out_weight.shape[1]
    columns = model_width // tp_count
    head_count = width // HD
    flat_k = cache_keys.reshape(req_count * cache_len, width)
    flat_v = cache_values.reshape(req_count * cache_len, width)

    def kernel(len_ref, q_ref, nk_ref, nv_ref, ck_ref, cv_ref, ow_ref, out_ref):
        row = lax.broadcasted_iota(jnp.int32, (tokens, 1), 0)
        lo = jnp.zeros((tokens, 1), jnp.int32)
        hi = jnp.zeros((tokens, 1), jnp.int32)
        first = jnp.zeros((tokens, 1), jnp.int32)
        for r in range(req_count):
            mine = (row >= r * POS) & (row < (r + 1) * POS)
            lo = jnp.where(mine, r * cache_len, lo)
            hi = jnp.where(mine, r * cache_len + len_ref[r], hi)
            first = jnp.where(mine, r * POS, first)
        key_at = lax.broadcasted_iota(jnp.int32, (tokens, req_count * cache_len), 1)
        live_c = (key_at >= lo) & (key_at < hi)
        fresh_at = lax.broadcasted_iota(jnp.int32, (tokens, tokens), 1)
        live_n = (fresh_at >= first) & (fresh_at <= row)
        dims = (((1,), (1,)), ((), ()))
        heads = []
        for h in range(head_count):
            cols = slice(h * HD, (h + 1) * HD)
            q = q_ref[:, cols]
            sc = lax.dot_general(q, ck_ref[:, cols], dims, preferred_element_type=jnp.float32) * HD ** (-0.5)
            sn = lax.dot_general(q, nk_ref[:, cols], dims, preferred_element_type=jnp.float32) * HD ** (-0.5)
            sc = jnp.where(live_c, sc, -1e30)
            sn = jnp.where(live_n, sn, -1e30)
            top = jnp.maximum(jnp.max(sc, axis=1, keepdims=True), jnp.max(sn, axis=1, keepdims=True))
            ec = jnp.exp(sc - top)
            en = jnp.exp(sn - top)
            total = jnp.sum(ec, axis=1, keepdims=True) + jnp.sum(en, axis=1, keepdims=True)
            wc = (ec / total).astype(jnp.bfloat16)
            wn = (en / total).astype(jnp.bfloat16)
            att = jnp.dot(wc, cv_ref[:, cols], preferred_element_type=jnp.float32)
            att = att + jnp.dot(wn, nv_ref[:, cols], preferred_element_type=jnp.float32)
            heads.append(att.astype(jnp.bfloat16))
        attended = jnp.concatenate(heads, axis=1)
        partial = jnp.dot(attended, ow_ref[...], preferred_element_type=jnp.float32)
        half = columns // 2
        for k in range(tp_count):
            out_ref[k, 0:tokens, :] = partial[:, k * columns:k * columns + half]
            out_ref[k, tokens:2 * tokens, :] = partial[:, k * columns + half:(k + 1) * columns]

    vmem = pl.BlockSpec(memory_space=pltpu.VMEM)
    return pl.pallas_call(
        kernel,
        out_shape=jax.ShapeDtypeStruct((tp_count, 2 * tokens, columns // 2), jnp.float32),
        in_specs=[pl.BlockSpec(memory_space=pltpu.SMEM)] + [vmem] * 6,
        out_specs=vmem,
    )(cache_lengths, queries, new_keys, new_values, flat_k, flat_v, out_weight)


def expert_apply(slot_rows, gate_weight, up_weight, down_weight):
    gated = jnp.einsum("secd,edf->secf", slot_rows, gate_weight, preferred_element_type=jnp.float32)
    upward = jnp.einsum("secd,edf->secf", slot_rows, up_weight, preferred_element_type=jnp.float32)
    activation = (jax.nn.silu(gated) * upward).astype(jnp.bfloat16)
    slots = activation.shape[0] * activation.shape[1] * activation.shape[2]
    hidden = activation.shape[3]
    width = down_weight.shape[2]
    return jnp.einsum(
        "sf,fkl->skl",
        activation.reshape(slots, hidden),
        down_weight.reshape(hidden, width // 128, 128),
        preferred_element_type=jnp.float32,
    )


def stack_halves(value):
    half = value.shape[1] // 2
    return jnp.concatenate([value[:, :half], value[:, half:]], axis=0)


def unstack_halves(value):
    rows = value.shape[0] // 2
    return jnp.concatenate([value[:rows], value[rows:]], axis=1)


def scatter_sum(value, tp_count):
    rows, width = value.shape
    pieces = value.reshape(rows, tp_count, 2, width // tp_count // 2).transpose(1, 2, 0, 3)
    pieces = pieces.reshape(tp_count, 2 * rows, width // tp_count // 2)
    pieces = lax.all_to_all(pieces, "tp", split_axis=0, concat_axis=0, tiled=True)
    return unstack_halves(jnp.sum(pieces.astype(jnp.float32), axis=0))


def gather_cols(value, tp_count):
    rows, columns = value.shape
    stacked = stack_halves(value)
    pieces = jnp.broadcast_to(stacked[None], (tp_count,) + stacked.shape)
    pieces = lax.all_to_all(pieces, "tp", split_axis=0, concat_axis=0, tiled=True)
    pieces = pieces.reshape(tp_count, 2, rows, columns // 2).transpose(2, 0, 1, 3)
    return pieces.reshape(rows, tp_count * columns)


def local(
    queries,
    new_keys,
    new_values,
    cache_keys,
    cache_values,
    cache_lengths,
    hidden_in,
    out_weight,
    norm_gain,
    routes,
    route_gates,
    gate_weight,
    up_weight,
    down_weight,
):
    model_width = out_weight.shape[1]
    tp_count = lax.axis_size("tp")
    pieces = attend_project(
        queries, new_keys, new_values, cache_keys, cache_values, cache_lengths, out_weight, tp_count
    )
    columns = model_width // tp_count
    offset = lax.axis_index("tp") * columns
    holders = lax.axis_size("req")
    dispatch, combine, slot_ids = slot_tables(routes, route_gates)
    hidden_cols = lax.dynamic_slice_in_dim(hidden_in, offset, columns, 1).astype(jnp.float32)
    pieces = lax.all_to_all(pieces, "tp", split_axis=0, concat_axis=0, tiled=True)
    summed_cols = unstack_halves(jnp.sum(pieces, axis=0)) + hidden_cols
    summed = gather_cols(summed_cols, tp_count)
    mean_square = jnp.mean(summed * summed, axis=-1, keepdims=True)
    normed = (summed * lax.rsqrt(mean_square + 1e-06) * norm_gain[None, :]).astype(jnp.bfloat16)
    token_count = normed.shape[0]
    slot_token = jnp.dot(
        dispatch, jnp.arange(1, token_count + 1, dtype=jnp.bfloat16), preferred_element_type=jnp.float32
    ).astype(jnp.int32)
    row_tiles = jnp.concatenate(
        [jnp.zeros((1, model_width // 128, 128), normed.dtype), normed.reshape(token_count, model_width // 128, 128)]
    )
    outbound = jnp.take(row_tiles, slot_token, axis=0, mode="clip")
    packed = (holders, CAP * model_width // 128, 128)
    outbound = outbound.reshape(packed)
    arrived = lax.all_to_all(outbound, "req", split_axis=0, concat_axis=0, tiled=True)
    produced = expert_apply(
        arrived.reshape(holders, 1, CAP, model_width),
        gate_weight,
        up_weight,
        down_weight,
    )
    returned = lax.all_to_all(
        produced.astype(jnp.bfloat16).reshape(packed), "req", split_axis=0, concat_axis=0, tiled=True
    )
    route_rows = jnp.take(
        returned.reshape(holders * CAP, model_width // 128, 128), slot_ids.reshape(-1), axis=0, mode="clip"
    )
    route_rows = route_rows.reshape(routes.shape + (model_width // 128, 128)).astype(jnp.float32)
    expert_sum = jnp.sum(route_rows * route_gates[:, :, None, None], axis=1).reshape(-1, model_width)
    expert_cols = scatter_sum(expert_sum.astype(jnp.bfloat16), tp_count)
    return (summed_cols + expert_cols).astype(jnp.bfloat16)


def solution(mesh):
    in_specs = (
        P("req", "tp"),
        P("req", "tp"),
        P("req", "tp"),
        P("req", None, "tp"),
        P("req", None, "tp"),
        P("req"),
        P("req", None),
        P("tp", None),
        P(),
        P("req", None),
        P("req", None),
        P("req", None, "tp"),
        P("req", None, "tp"),
        P("req", "tp", None),
    )
    out_specs = P("req", "tp")
    return jax.shard_map(local, mesh=mesh, in_specs=in_specs, out_specs=out_specs, check_vma=False)
```

```python
import jax
import jax.numpy as jnp
from jax import lax
from jax.experimental import pallas as pl
from jax.experimental.pallas import tpu as pltpu
from jax.sharding import PartitionSpec as P

HD = 128
EXPERTS = 64
POS = 5
CACHE = 384
CAP = 3


def slot_tables(local_routes, local_gates):
    flat_routes = local_routes.reshape(-1)
    expert_ids = jnp.arange(EXPERTS, dtype=jnp.int32)
    onehot = (flat_routes[:, None] == expert_ids[None, :]).astype(jnp.int32)
    before = jnp.cumsum(onehot, axis=0) - onehot
    ranks = jnp.sum(before * onehot, axis=1)
    slot_ids = (flat_routes * CAP + ranks).reshape(local_routes.shape)
    slot_range = jnp.arange(EXPERTS * CAP, dtype=jnp.int32)
    matches = slot_ids[None, :, :] == slot_range[:, None, None]
    dispatch = jnp.any(matches, axis=-1).astype(jnp.bfloat16)
    combine = jnp.sum(jnp.where(matches, local_gates[None, :, :], 0.0), axis=-1).T
    return (dispatch, combine)


def attend_project(queries, new_keys, new_values, cache_keys, cache_values, cache_lengths, out_weight, tp_count):
    req_count, cache_len, width = cache_keys.shape
    tokens = queries.shape[0]
    model_width = out_weight.shape[1]
    columns = model_width // tp_count
    head_count = width // HD
    flat_k = cache_keys.reshape(req_count * cache_len, width)
    flat_v = cache_values.reshape(req_count * cache_len, width)

    def kernel(len_ref, q_ref, nk_ref, nv_ref, ck_ref, cv_ref, ow_ref, out_ref):
        head = pl.program_id(0)
        row = lax.broadcasted_iota(jnp.int32, (tokens, 1), 0)
        lo = jnp.zeros((tokens, 1), jnp.int32)
        hi = jnp.zeros((tokens, 1), jnp.int32)
        first = jnp.zeros((tokens, 1), jnp.int32)
        for r in range(req_count):
            mine = (row >= r * POS) & (row < (r + 1) * POS)
            lo = jnp.where(mine, r * cache_len, lo)
            hi = jnp.where(mine, r * cache_len + len_ref[r], hi)
            first = jnp.where(mine, r * POS, first)
        key_at = lax.broadcasted_iota(jnp.int32, (tokens, req_count * cache_len), 1)
        live_c = (key_at >= lo) & (key_at < hi)
        fresh_at = lax.broadcasted_iota(jnp.int32, (tokens, tokens), 1)
        live_n = (fresh_at >= first) & (fresh_at <= row)
        dims = (((1,), (1,)), ((), ()))
        q = q_ref[...]
        sc = lax.dot_general(q, ck_ref[...], dims, preferred_element_type=jnp.float32) * HD ** (-0.5)
        sn = lax.dot_general(q, nk_ref[...], dims, preferred_element_type=jnp.float32) * HD ** (-0.5)
        sc = jnp.where(live_c, sc, -1e30)
        sn = jnp.where(live_n, sn, -1e30)
        top = jnp.maximum(jnp.max(sc, axis=1, keepdims=True), jnp.max(sn, axis=1, keepdims=True))
        ec = jnp.exp(sc - top)
        en = jnp.exp(sn - top)
        total = jnp.sum(ec, axis=1, keepdims=True) + jnp.sum(en, axis=1, keepdims=True)
        wc = (ec / total).astype(jnp.bfloat16)
        wn = (en / total).astype(jnp.bfloat16)
        att = jnp.dot(wc, cv_ref[...], preferred_element_type=jnp.float32)
        att = att + jnp.dot(wn, nv_ref[...], preferred_element_type=jnp.float32)
        partial = jnp.dot(att.astype(jnp.bfloat16), ow_ref[...], preferred_element_type=jnp.float32)
        half = columns // 2

        @pl.when(head == 0)
        def _():
            for k in range(tp_count):
                out_ref[k, 0:tokens, :] = partial[:, k * columns:k * columns + half]
                out_ref[k, tokens:2 * tokens, :] = partial[:, k * columns + half:(k + 1) * columns]

        @pl.when(head > 0)
        def _():
            for k in range(tp_count):
                out_ref[k, 0:tokens, :] += partial[:, k * columns:k * columns + half]
                out_ref[k, tokens:2 * tokens, :] += partial[:, k * columns + half:(k + 1) * columns]

    token_block = pl.BlockSpec((tokens, HD), lambda h: (0, h))
    cache_block = pl.BlockSpec((req_count * cache_len, HD), lambda h: (0, h))
    return pl.pallas_call(
        kernel,
        grid=(head_count,),
        out_shape=jax.ShapeDtypeStruct((tp_count, 2 * tokens, columns // 2), jnp.float32),
        in_specs=[
            pl.BlockSpec(memory_space=pltpu.SMEM),
            token_block,
            token_block,
            token_block,
            cache_block,
            cache_block,
            pl.BlockSpec((HD, model_width), lambda h: (h, 0)),
        ],
        out_specs=pl.BlockSpec((tp_count, 2 * tokens, columns // 2), lambda h: (0, 0, 0)),
    )(cache_lengths, queries, new_keys, new_values, flat_k, flat_v, out_weight)


def expert_apply(slot_rows, gate_weight, up_weight, down_weight):
    gated = jnp.einsum("secd,edf->secf", slot_rows, gate_weight, preferred_element_type=jnp.float32)
    upward = jnp.einsum("secd,edf->secf", slot_rows, up_weight, preferred_element_type=jnp.float32)
    activation = (jax.nn.silu(gated) * upward).astype(jnp.bfloat16)
    slots = activation.shape[0] * activation.shape[1] * activation.shape[2]
    hidden = activation.shape[3]
    width = down_weight.shape[2]
    return jnp.einsum(
        "sf,fkl->skl",
        activation.reshape(slots, hidden),
        down_weight.reshape(hidden, width // 128, 128),
        preferred_element_type=jnp.float32,
    )


def stack_halves(value):
    half = value.shape[1] // 2
    return jnp.concatenate([value[:, :half], value[:, half:]], axis=0)


def unstack_halves(value):
    rows = value.shape[0] // 2
    return jnp.concatenate([value[:rows], value[rows:]], axis=1)


def scatter_sum(value, tp_count):
    rows, width = value.shape
    pieces = value.reshape(rows, tp_count, 2, width // tp_count // 2).transpose(1, 2, 0, 3)
    pieces = pieces.reshape(tp_count, 2 * rows, width // tp_count // 2)
    pieces = lax.all_to_all(pieces, "tp", split_axis=0, concat_axis=0, tiled=True)
    return unstack_halves(jnp.sum(pieces.astype(jnp.float32), axis=0))


def gather_cols(value, tp_count):
    rows, columns = value.shape
    stacked = stack_halves(value)
    pieces = jnp.broadcast_to(stacked[None], (tp_count,) + stacked.shape)
    pieces = lax.all_to_all(pieces, "tp", split_axis=0, concat_axis=0, tiled=True)
    pieces = pieces.reshape(tp_count, 2, rows, columns // 2).transpose(2, 0, 1, 3)
    return pieces.reshape(rows, tp_count * columns)


def local(
    queries,
    new_keys,
    new_values,
    cache_keys,
    cache_values,
    cache_lengths,
    hidden_in,
    out_weight,
    norm_gain,
    routes,
    route_gates,
    gate_weight,
    up_weight,
    down_weight,
):
    model_width = out_weight.shape[1]
    tp_count = lax.axis_size("tp")
    pieces = attend_project(
        queries, new_keys, new_values, cache_keys, cache_values, cache_lengths, out_weight, tp_count
    )
    columns = model_width // tp_count
    offset = lax.axis_index("tp") * columns
    holders = lax.axis_size("req")
    dispatch, combine = slot_tables(routes, route_gates)
    hidden_cols = lax.dynamic_slice_in_dim(hidden_in, offset, columns, 1).astype(jnp.float32)
    pieces = lax.all_to_all(pieces, "tp", split_axis=0, concat_axis=0, tiled=True)
    summed_cols = unstack_halves(jnp.sum(pieces, axis=0)) + hidden_cols
    summed = gather_cols(summed_cols, tp_count)
    mean_square = jnp.mean(summed * summed, axis=-1, keepdims=True)
    normed = (summed * lax.rsqrt(mean_square + 1e-06) * norm_gain[None, :]).astype(jnp.bfloat16)
    token_count = normed.shape[0]
    slot_token = jnp.dot(
        dispatch, jnp.arange(1, token_count + 1, dtype=jnp.bfloat16), preferred_element_type=jnp.float32
    ).astype(jnp.int32)
    row_tiles = jnp.concatenate(
        [jnp.zeros((1, model_width // 128, 128), normed.dtype), normed.reshape(token_count, model_width // 128, 128)]
    )
    outbound = jnp.take(row_tiles, slot_token, axis=0, mode="clip")
    packed = (holders, CAP * model_width // 128, 128)
    outbound = outbound.reshape(packed)
    arrived = lax.all_to_all(outbound, "req", split_axis=0, concat_axis=0, tiled=True)
    produced = expert_apply(
        arrived.reshape(holders, 1, CAP, model_width),
        gate_weight,
        up_weight,
        down_weight,
    )
    returned = lax.all_to_all(
        produced.astype(jnp.bfloat16).reshape(packed), "req", split_axis=0, concat_axis=0, tiled=True
    ).astype(jnp.float32)
    expert_sum = jnp.dot(
        combine,
        returned.reshape(-1, model_width),
        precision=lax.Precision.HIGHEST,
        preferred_element_type=jnp.float32,
    )
    expert_cols = scatter_sum(expert_sum.astype(jnp.bfloat16), tp_count)
    return (summed_cols + expert_cols).astype(jnp.bfloat16)


def solution(mesh):
    in_specs = (
        P("req", "tp"),
        P("req", "tp"),
        P("req", "tp"),
        P("req", None, "tp"),
        P("req", None, "tp"),
        P("req"),
        P("req", None),
        P("tp", None),
        P(),
        P("req", None),
        P("req", None),
        P("req", None, "tp"),
        P("req", None, "tp"),
        P("req", "tp", None),
    )
    out_specs = P("req", "tp")
    return jax.shard_map(local, mesh=mesh, in_specs=in_specs, out_specs=out_specs, check_vma=False)
```

```python
import jax
import jax.numpy as jnp
from jax import lax
from jax.experimental import pallas as pl
from jax.experimental.pallas import tpu as pltpu
from jax.sharding import PartitionSpec as P

HD = 128
EXPERTS = 64
POS = 5
CACHE = 384
CAP = 3


def slot_tables(local_routes, local_gates):
    flat_routes = local_routes.reshape(-1)
    expert_ids = jnp.arange(EXPERTS, dtype=jnp.int32)
    onehot = (flat_routes[:, None] == expert_ids[None, :]).astype(jnp.int32)
    before = jnp.cumsum(onehot, axis=0) - onehot
    ranks = jnp.sum(before * onehot, axis=1)
    slot_ids = (flat_routes * CAP + ranks).reshape(local_routes.shape)
    slot_range = jnp.arange(EXPERTS * CAP, dtype=jnp.int32)
    matches = slot_ids[None, :, :] == slot_range[:, None, None]
    dispatch = jnp.any(matches, axis=-1).astype(jnp.bfloat16)
    combine = jnp.sum(jnp.where(matches, local_gates[None, :, :], 0.0), axis=-1).T
    return (dispatch, combine)


def attend_project(queries, new_keys, new_values, cache_keys, cache_values, cache_lengths, out_weight, tp_count, hidden_in, me):
    req_count, cache_len, width = cache_keys.shape
    tokens = queries.shape[0]
    model_width = out_weight.shape[1]
    columns = model_width // tp_count
    head_count = width // HD
    flat_k = cache_keys.reshape(req_count * cache_len, width)
    flat_v = cache_values.reshape(req_count * cache_len, width)

    def kernel(len_ref, me_ref, q_ref, nk_ref, nv_ref, ck_ref, cv_ref, ow_ref, hid_ref, out_ref):
        row = lax.broadcasted_iota(jnp.int32, (tokens, 1), 0)
        lo = jnp.zeros((tokens, 1), jnp.int32)
        hi = jnp.zeros((tokens, 1), jnp.int32)
        first = jnp.zeros((tokens, 1), jnp.int32)
        for r in range(req_count):
            mine = (row >= r * POS) & (row < (r + 1) * POS)
            lo = jnp.where(mine, r * cache_len, lo)
            hi = jnp.where(mine, r * cache_len + len_ref[r], hi)
            first = jnp.where(mine, r * POS, first)
        key_at = lax.broadcasted_iota(jnp.int32, (tokens, req_count * cache_len), 1)
        live_c = (key_at >= lo) & (key_at < hi)
        fresh_at = lax.broadcasted_iota(jnp.int32, (tokens, tokens), 1)
        live_n = (fresh_at >= first) & (fresh_at <= row)
        dims = (((1,), (1,)), ((), ()))
        heads = []
        for h in range(head_count):
            cols = slice(h * HD, (h + 1) * HD)
            q = q_ref[:, cols]
            sc = lax.dot_general(q, ck_ref[:, cols], dims, preferred_element_type=jnp.float32) * HD ** (-0.5)
            sn = lax.dot_general(q, nk_ref[:, cols], dims, preferred_element_type=jnp.float32) * HD ** (-0.5)
            sc = jnp.where(live_c, sc, -1e30)
            sn = jnp.where(live_n, sn, -1e30)
            top = jnp.maximum(jnp.max(sc, axis=1, keepdims=True), jnp.max(sn, axis=1, keepdims=True))
            ec = jnp.exp(sc - top)
            en = jnp.exp(sn - top)
            total = jnp.sum(ec, axis=1, keepdims=True) + jnp.sum(en, axis=1, keepdims=True)
            wc = (ec / total).astype(jnp.bfloat16)
            wn = (en / total).astype(jnp.bfloat16)
            att = jnp.dot(wc, cv_ref[:, cols], preferred_element_type=jnp.float32)
            att = att + jnp.dot(wn, nv_ref[:, cols], preferred_element_type=jnp.float32)
            heads.append(att.astype(jnp.bfloat16))
        attended = jnp.concatenate(heads, axis=1)
        partial = jnp.dot(attended, ow_ref[...], preferred_element_type=jnp.float32)
        half = columns // 2
        for k in range(tp_count):
            own = jnp.where(me_ref[0] == k, 1.0, 0.0)
            lo_cols = slice(k * columns, k * columns + half)
            hi_cols = slice(k * columns + half, (k + 1) * columns)
            out_ref[k, 0:tokens, :] = partial[:, lo_cols] + own * hid_ref[:, lo_cols].astype(jnp.float32)
            out_ref[k, tokens:2 * tokens, :] = partial[:, hi_cols] + own * hid_ref[:, hi_cols].astype(jnp.float32)

    vmem = pl.BlockSpec(memory_space=pltpu.VMEM)
    return pl.pallas_call(
        kernel,
        out_shape=jax.ShapeDtypeStruct((tp_count, 2 * tokens, columns // 2), jnp.float32),
        in_specs=[pl.BlockSpec(memory_space=pltpu.SMEM)] * 2 + [vmem] * 7,
        out_specs=vmem,
    )(cache_lengths, me, queries, new_keys, new_values, flat_k, flat_v, out_weight, hidden_in)


def expert_apply(slot_rows, gate_weight, up_weight, down_weight):
    gated = jnp.einsum("secd,edf->secf", slot_rows, gate_weight, preferred_element_type=jnp.float32)
    upward = jnp.einsum("secd,edf->secf", slot_rows, up_weight, preferred_element_type=jnp.float32)
    activation = (jax.nn.silu(gated) * upward).astype(jnp.bfloat16)
    slots = activation.shape[0] * activation.shape[1] * activation.shape[2]
    hidden = activation.shape[3]
    width = down_weight.shape[2]
    return jnp.einsum(
        "sf,fkl->skl",
        activation.reshape(slots, hidden),
        down_weight.reshape(hidden, width // 128, 128),
        preferred_element_type=jnp.float32,
    )


def stack_halves(value):
    half = value.shape[1] // 2
    return jnp.concatenate([value[:, :half], value[:, half:]], axis=0)


def unstack_halves(value):
    rows = value.shape[0] // 2
    return jnp.concatenate([value[:rows], value[rows:]], axis=1)


def scatter_sum(value, tp_count):
    rows, width = value.shape
    pieces = value.reshape(rows, tp_count, 2, width // tp_count // 2).transpose(1, 2, 0, 3)
    pieces = pieces.reshape(tp_count, 2 * rows, width // tp_count // 2)
    pieces = lax.all_to_all(pieces, "tp", split_axis=0, concat_axis=0, tiled=True)
    return unstack_halves(jnp.sum(pieces.astype(jnp.float32), axis=0))


def gather_cols(value, tp_count):
    rows, columns = value.shape
    stacked = stack_halves(value)
    pieces = jnp.broadcast_to(stacked[None], (tp_count,) + stacked.shape)
    pieces = lax.all_to_all(pieces, "tp", split_axis=0, concat_axis=0, tiled=True)
    pieces = pieces.reshape(tp_count, 2, rows, columns // 2).transpose(2, 0, 1, 3)
    return pieces.reshape(rows, tp_count * columns)


def local(
    queries,
    new_keys,
    new_values,
    cache_keys,
    cache_values,
    cache_lengths,
    hidden_in,
    out_weight,
    norm_gain,
    routes,
    route_gates,
    gate_weight,
    up_weight,
    down_weight,
):
    model_width = out_weight.shape[1]
    tp_count = lax.axis_size("tp")
    pieces = attend_project(
        queries, new_keys, new_values, cache_keys, cache_values, cache_lengths, out_weight, tp_count,
        hidden_in, lax.axis_index("tp").astype(jnp.int32).reshape(1),
    )
    columns = model_width // tp_count
    offset = lax.axis_index("tp") * columns
    holders = lax.axis_size("req")
    dispatch, combine = slot_tables(routes, route_gates)
    hidden_cols = lax.dynamic_slice_in_dim(hidden_in, offset, columns, 1).astype(jnp.float32)
    pieces = lax.all_to_all(pieces, "tp", split_axis=0, concat_axis=0, tiled=True)
    summed_cols = unstack_halves(jnp.sum(pieces, axis=0))
    summed = gather_cols(summed_cols, tp_count)
    mean_square = jnp.mean(summed * summed, axis=-1, keepdims=True)
    normed = (summed * lax.rsqrt(mean_square + 1e-06) * norm_gain[None, :]).astype(jnp.bfloat16)
    token_count = normed.shape[0]
    slot_token = jnp.dot(
        dispatch, jnp.arange(1, token_count + 1, dtype=jnp.bfloat16), preferred_element_type=jnp.float32
    ).astype(jnp.int32)
    row_tiles = jnp.concatenate(
        [jnp.zeros((1, model_width // 128, 128), normed.dtype), normed.reshape(token_count, model_width // 128, 128)]
    )
    outbound = jnp.take(row_tiles, slot_token, axis=0, mode="clip")
    packed = (holders, CAP * model_width // 128, 128)
    outbound = outbound.reshape(packed)
    arrived = lax.all_to_all(outbound, "req", split_axis=0, concat_axis=0, tiled=True)
    produced = expert_apply(
        arrived.reshape(holders, 1, CAP, model_width),
        gate_weight,
        up_weight,
        down_weight,
    )
    returned = lax.all_to_all(
        produced.astype(jnp.bfloat16).reshape(packed), "req", split_axis=0, concat_axis=0, tiled=True
    ).astype(jnp.float32)
    expert_sum = jnp.dot(
        combine,
        returned.reshape(-1, model_width),
        precision=lax.Precision.HIGHEST,
        preferred_element_type=jnp.float32,
    )
    expert_cols = scatter_sum(expert_sum.astype(jnp.bfloat16), tp_count)
    return (summed_cols + expert_cols).astype(jnp.bfloat16)


def solution(mesh):
    in_specs = (
        P("req", "tp"),
        P("req", "tp"),
        P("req", "tp"),
        P("req", None, "tp"),
        P("req", None, "tp"),
        P("req"),
        P("req", None),
        P("tp", None),
        P(),
        P("req", None),
        P("req", None),
        P("req", None, "tp"),
        P("req", None, "tp"),
        P("req", "tp", None),
    )
    out_specs = P("req", "tp")
    return jax.shard_map(local, mesh=mesh, in_specs=in_specs, out_specs=out_specs, check_vma=False)
```
